256 devices in a mesh: dp: 32 (over y, z), tensor: 8 (over x, core).
Axes of the slice: x: 4, y: 4, z: 8, core: 2. Of those that a mesh axis runs over, the one named last changes fastest.
Arguments:
- hidden_in: bfloat16 [1024, 8192], P('dp'), may hold values from -40 to 40
- norm_gain: bfloat16 [8192], P('dp'), may hold values from 0.25 to 2.5
- query_weight: bfloat16 [8192, 8192], P('dp', 'tensor'), may hold values from -0.0625 to 0.0625
- key_weight: bfloat16 [8192, 1024], P('dp', 'tensor'), may hold values from -0.0625 to 0.0625
- value_weight: bfloat16 [8192, 1024], P('dp', 'tensor'), may hold values from -0.0625 to 0.0625
- output_weight: bfloat16 [8192, 8192], P('tensor', 'dp'), may hold values from -0.25 to 0.25
- key_value_cache: bfloat16 [1024, 256, 2, 8, 128], P('dp', None, None, 'tensor'), may hold values from -150 to 150, as said below
- cache_lengths: int32 [1024], replicated, may hold values from 2 to 256, as said below
- parent_beam: int32 [1024], replicated, may hold values from 0 to 1023, as said below
- beam_alive: int32 [1024], replicated, may hold values 0 or 1
Outputs:
- attention_out: bfloat16 [1024, 8192], P(None, 'dp')
The draws below stay inside these ranges and needn't reach their ends.
Inputs may be any that keep to these rules, and one draw needn't show every extreme that they name: `parent_beam`: among the beams of one device, at most 2 have parents that lie on any one device (beam i lies on device i // 32); on every device some device holds exactly 2 of their parents. `cache_lengths`: some beam holds exactly 256 tokens. `key_value_cache`: slots at or past a beam's length hold arbitrary values.
All inputs are finite; a program needn't handle non-finite values.
Results may differ from the reference program's by a relative error of at most 0.012.
Values may be sent and summed in bfloat16 or wider, within the bound.
No kernel may reach another device: no remote copies, remote signals or barrier semaphores. Data moves between devices by JAX's collectives and lax.ppermute only.
A program may use at most 128 MiB of HBM per device.

```python
import math
import jax
import jax.numpy as jnp
from jax import lax

D = 8192
HEADS = 64
KV_HEADS = 8
HEAD_DIM = 128
BEAM_DEV = 32
CACHE_LEN = 256
BEAMS = 1024
CAP = 2
N_DP = 32


def draw_hidden_in(key, part):
    first_key, second_key, third_key = jax.random.split(key, 3)
    row_scale = jnp.exp(jax.random.uniform(first_key, (BEAMS, 1), jnp.float32, math.log(0.3), math.log(3.0)))
    column_scale = jnp.exp(jax.random.uniform(second_key, (1, D), jnp.float32, math.log(0.3), math.log(3.0)))
    base_values = jnp.clip(jax.random.normal(third_key, (BEAMS, D), jnp.float32), -4.0, 4.0)
    return (base_values * row_scale * column_scale).astype(jnp.bfloat16)


def draw_key_value_cache(key, part):
    first_key = jax.random.fold_in(key, 0)
    full_shape = (BEAMS, CACHE_LEN, 2, KV_HEADS, HEAD_DIM)
    base_values = jnp.clip(jax.random.normal(first_key, full_shape, jnp.float32), -5.0, 5.0)
    return base_values.astype(jnp.bfloat16)


def draw_cache_lengths(key, part):
    first_key, second_key = jax.random.split(key, 2)
    drawn = jax.random.randint(first_key, (BEAMS,), 2, CACHE_LEN + 1)
    longest = jax.random.randint(second_key, (), 0, BEAMS)
    return jnp.where(jnp.arange(BEAMS) == longest, CACHE_LEN, drawn).astype(jnp.int32)


def draw_parent_beam(key, part):

    def one_device(device):
        device_key = jax.random.fold_in(key, device)
        first_key, second_key, third_key = jax.random.split(device_key, 3)
        ordering = jax.random.permutation(first_key, N_DP)
        grouped = ordering[jnp.arange(BEAM_DEV) // CAP]
        shuffled = jax.random.permutation(second_key, grouped)
        within = jax.random.randint(third_key, (BEAM_DEV,), 0, BEAM_DEV)
        return shuffled * BEAM_DEV + within
    return jax.vmap(one_device)(jnp.arange(N_DP)).reshape(-1).astype(jnp.int32)


def set_ends(values, own_key, smallest, high):
    index_at = [jax.random.randint(jax.random.fold_in(own_key, axis), (), 0, length) for axis, length in enumerate(values.shape)]
    main_axis = values.shape.index(max(values.shape))
    beside = index_at[:main_axis] + [(index_at[main_axis] + 1) % values.shape[main_axis]] + index_at[main_axis + 1:]
    return values.at[tuple(index_at)].set(smallest).at[tuple(beside)].set(high)


def levels(stream_key, shape, cuts, least, top_value):
    factor_of, own = 1.0, jax.random.fold_in(stream_key, 6)
    for dim, parts in cuts:
        heights = jnp.exp(jax.random.uniform(jax.random.fold_in(own, dim), (parts,), jnp.float32, least / len(cuts), top_value / len(cuts)))
        factor_of = factor_of * jnp.repeat(heights, shape[dim] // parts).reshape([-1 if axis == dim else 1 for axis in range(len(shape))])
    return factor_of


def bell_draw(own_key, shape, deviation, limit, cuts=(), kind=jnp.bfloat16):
    entries = deviation * jax.random.normal(own_key, shape, jnp.float32)
    if cuts:
        entries = entries * levels(own_key, shape, cuts, -0.22, 0.18)
    return jnp.clip(entries, -limit, limit).astype(kind)


def setup_inputs(seed: int = 0) -> dict:
    keys = jax.random.split(jax.random.key(seed), 11)
    hidden_in = draw_hidden_in(jax.random.fold_in(keys[10], 71), 0)
    norm_gain = jnp.clip(jnp.exp(math.log(2.5) - 2.3025851 * jax.random.uniform(keys[1], (D,), jnp.float32) ** levels(keys[1], (D,), ((0, 32),), -0.2, 0.2)), 0.25, 2.5).astype(jnp.bfloat16)
    query_weight = bell_draw(keys[2], (D, HEADS * HEAD_DIM), D ** -0.5, 0.0625, ((0, 32), (1, 8)))
    key_weight = bell_draw(keys[3], (D, KV_HEADS * HEAD_DIM), D ** -0.5, 0.0625, ((0, 32), (1, 8)))
    value_weight = bell_draw(keys[4], (D, KV_HEADS * HEAD_DIM), D ** -0.5, 0.0625, ((0, 32), (1, 8)))
    output_weight = bell_draw(keys[5], (HEADS * HEAD_DIM, D), (HEADS * HEAD_DIM // 16) ** -0.5, 0.25, ((0, 8), (1, 32)))
    key_value_cache = draw_key_value_cache(jax.random.fold_in(keys[10], 71), 0)
    cache_lengths = draw_cache_lengths(jax.random.fold_in(keys[10], 71), 0)
    parent_beam = draw_parent_beam(jax.random.fold_in(keys[10], 71), 0)
    beam_alive = set_ends((jax.random.randint(keys[9], (BEAMS,), 0, 8) < 7).astype(jnp.int32), jax.random.fold_in(keys[9], 1), 0, 1)
    return {"hidden_in": hidden_in, "norm_gain": norm_gain, "query_weight": query_weight, "key_weight": key_weight, "value_weight": value_weight, "output_weight": output_weight, "key_value_cache": key_value_cache, "cache_lengths": cache_lengths, "parent_beam": parent_beam, "beam_alive": beam_alive}


def rotate(vectors, position):
    half_width = vectors.shape[-1] // 2
    pair_index = jnp.arange(half_width).astype(jnp.float32)
    frequency = jnp.exp(pair_index * (-2.0 * math.log(1000000.0) / vectors.shape[-1]))
    angles = position.astype(jnp.float32)[:, None] * frequency[None, :]
    cosine = jnp.cos(angles)[:, None, :]
    sine_part = jnp.sin(angles)[:, None, :]
    first_half = vectors[..., :half_width]
    second = vectors[..., half_width:]
    return jnp.concatenate([first_half * cosine - second * sine_part, second * cosine + first_half * sine_part], axis=-1)

def attend(queries, key_rows, value_rows, key_new, value_new, length_row):
    row_count, head_total, head_width = queries.shape
    groups = key_rows.shape[2]
    length = key_rows.shape[1]
    grouped = queries.astype(jnp.float32).reshape(row_count, groups, head_total // groups, head_width)
    score_scale = 1.0 / math.sqrt(head_width)
    cached = jnp.einsum('rkgd,rlkd->rkgl', grouped, key_rows.astype(jnp.float32)) * score_scale
    latest = jnp.einsum('rkgd,rkd->rkg', grouped, key_new.astype(jnp.float32)) * score_scale
    is_valid = (jnp.arange(length, dtype=jnp.int32)[None, :] < length_row.astype(jnp.int32)[:, None])[:, None, None, :]
    cached = jnp.where(is_valid, cached, -jnp.inf)
    highest = jnp.maximum(lax.optimization_barrier(jnp.max(cached, axis=-1)), latest)
    cached_exp = jnp.exp(cached - highest[..., None])
    latest_exp = jnp.exp(latest - highest)
    denominator = lax.optimization_barrier(jnp.sum(cached_exp, axis=-1)) + latest_exp
    cached_weight = (cached_exp / denominator[..., None]).astype(jnp.bfloat16)
    latest_weight = (latest_exp / denominator).astype(jnp.bfloat16)
    mixture = jnp.einsum('rkgl,rlkd->rkgd', cached_weight.astype(jnp.float32), value_rows.astype(jnp.float32))
    mixture = mixture + latest_weight.astype(jnp.float32)[..., None] * value_new.astype(jnp.float32)[:, :, None, :]
    return mixture.reshape(row_count, head_total * head_width).astype(jnp.bfloat16)

def reference(hidden_in, norm_gain, query_weight, key_weight, value_weight, output_weight, key_value_cache, cache_lengths, parent_beam, beam_alive):
    hidden_float = hidden_in.astype(jnp.float32)
    inverse = lax.rsqrt(lax.optimization_barrier(jnp.mean(hidden_float * hidden_float, axis=1)) + 1e-06)
    scaled = (hidden_float * norm_gain.astype(jnp.float32)[None, :]).astype(jnp.bfloat16)
    position = jnp.take(cache_lengths, parent_beam)
    query_proj = jnp.dot(scaled, query_weight, preferred_element_type=jnp.float32) * inverse[:, None]
    key_proj = jnp.dot(scaled, key_weight, preferred_element_type=jnp.float32) * inverse[:, None]
    value_proj = jnp.dot(scaled, value_weight, preferred_element_type=jnp.float32) * inverse[:, None]
    queries = rotate(query_proj.reshape(BEAMS, HEADS, HEAD_DIM), position).astype(jnp.bfloat16)
    key_new = rotate(key_proj.reshape(BEAMS, KV_HEADS, HEAD_DIM), position).astype(jnp.bfloat16)
    value_new = value_proj.reshape(BEAMS, KV_HEADS, HEAD_DIM).astype(jnp.bfloat16)

    def one_beam(beam_items):
        query_row, key_row, value_row, parent_row, alive_row = beam_items
        cache_block = lax.dynamic_index_in_dim(key_value_cache, parent_row, 0, keepdims=True)
        length_one = lax.dynamic_index_in_dim(cache_lengths, parent_row, 0, keepdims=True)
        mixture = attend(query_row[None], cache_block[:, :, 0], cache_block[:, :, 1], key_row[None], value_row[None], length_one)
        return jnp.where(alive_row > 0, mixture[0], jnp.zeros_like(mixture[0]))
    attention = lax.map(one_beam, (queries, key_new, value_new, parent_beam, beam_alive))
    return jnp.dot(attention, output_weight, preferred_element_type=jnp.float32).astype(jnp.bfloat16)
```

```python
import functools
import math

import jax
import jax.numpy as jnp
from jax import lax
from jax.experimental import pallas as pl
from jax.experimental.pallas import tpu as pltpu
from jax.sharding import PartitionSpec as P

HEAD_DIM = 128
SLOTS_PER_STEP = 8


def rotate(vectors, position):
    half_width = vectors.shape[-1] // 2
    pair_index = jnp.arange(half_width).astype(jnp.float32)
    frequency = jnp.exp(pair_index * (-2.0 * math.log(1000000.0) / vectors.shape[-1]))
    angles = position.astype(jnp.float32)[:, None] * frequency[None, :]
    cosine = jnp.cos(angles)[:, None, :]
    sine_part = jnp.sin(angles)[:, None, :]
    first_half = vectors[..., :half_width]
    second = vectors[..., half_width:]
    return jnp.concatenate(
        [first_half * cosine - second * sine_part, second * cosine + first_half * sine_part],
        axis=-1,
    )


def arrival_ranks(sources):
    ordinal = jnp.arange(sources.shape[-1], dtype=jnp.int32)
    earlier = (sources[..., None, :] == sources[..., :, None]) & (
        ordinal[None, :] < ordinal[:, None]
    )
    return jnp.sum(earlier.astype(jnp.int32), axis=-1)


def attend_kernel(parent_ref, length_ref, packed_ref, *refs):
    cache_refs = refs[:-1]
    out_ref = refs[-1]
    group = len(cache_refs)
    step = pl.program_id(0)
    head_width = packed_ref.shape[-1]
    head_total = packed_ref.shape[1] - 2
    score_scale = 1.0 / math.sqrt(head_width)
    for g in range(group):
        length = length_ref[step * group + g]
        row = packed_ref[g].astype(jnp.float32)
        queries = row[:head_total].astype(jnp.bfloat16)
        key_new = row[head_total : head_total + 1]
        value_new = row[head_total + 1 : head_total + 2]
        block = cache_refs[g][0]
        keys = block[:, :head_width]
        values = block[:, head_width:]
        cached = (
            lax.dot_general(
                queries, keys, (((1,), (1,)), ((), ())), preferred_element_type=jnp.float32
            )
            * score_scale
        )
        latest = (
            jnp.sum(row[:head_total] * key_new, axis=-1, keepdims=True) * score_scale
        )
        slot = lax.broadcasted_iota(jnp.int32, cached.shape, 1)
        cached = jnp.where(slot < length, cached, -jnp.inf)
        highest = jnp.maximum(jnp.max(cached, axis=-1, keepdims=True), latest)
        cached_exp = jnp.exp(cached - highest)
        latest_exp = jnp.exp(latest - highest)
        denominator = jnp.sum(cached_exp, axis=-1, keepdims=True) + latest_exp
        cached_weight = (cached_exp / denominator).astype(jnp.bfloat16)
        latest_weight = (latest_exp / denominator).astype(jnp.bfloat16)
        mixture = jnp.dot(cached_weight, values, preferred_element_type=jnp.float32)
        mixture = mixture + latest_weight.astype(jnp.float32) * value_new
        out_ref[g] = mixture.astype(out_ref.dtype)


def attend_slots(packed, cache_rows, parents, lengths):
    slot_total, rows, head_width = packed.shape
    head_total = rows - 2
    group = SLOTS_PER_STEP
    cache_len, row_width = cache_rows.shape[1], cache_rows.shape[2]

    def cache_map(g):
        return lambda i, parent_ref, length_ref: (parent_ref[i * group + g], 0, 0)

    grid_spec = pltpu.PrefetchScalarGridSpec(
        num_scalar_prefetch=2,
        grid=(slot_total // group,),
        in_specs=[pl.BlockSpec((group, rows, head_width), lambda i, p, l: (i, 0, 0))]
        + [pl.BlockSpec((1, cache_len, row_width), cache_map(g)) for g in range(group)],
        out_specs=pl.BlockSpec((group, head_total, head_width), lambda i, p, l: (i, 0, 0)),
    )
    return pl.pallas_call(
        attend_kernel,
        grid_spec=grid_spec,
        out_shape=jax.ShapeDtypeStruct((slot_total, head_total, head_width), jnp.bfloat16),
    )(parents, lengths, packed, *([cache_rows] * group))


def body(
    hidden_in,
    norm_gain,
    query_weight,
    key_weight,
    value_weight,
    output_weight,
    key_value_cache,
    cache_lengths,
    parent_beam,
    beam_alive,
):
    device_count = lax.axis_size("dp")
    device_rank = lax.axis_index("dp")
    tensor_count = lax.axis_size("tensor")
    local_beams = hidden_in.shape[0]
    capacity = max(2, (2 * local_beams + device_count - 1) // device_count)
    slot_total = device_count * capacity

    hidden_float = hidden_in.astype(jnp.float32)
    inverse = lax.rsqrt(jnp.mean(hidden_float * hidden_float, axis=1) + 1e-06)
    blocked = lax.all_to_all(hidden_in, "dp", split_axis=1, concat_axis=0, tiled=True)
    scaled = (blocked.astype(jnp.float32) * norm_gain.astype(jnp.float32)[None, :]).astype(
        jnp.bfloat16
    )
    query_width = query_weight.shape[1]
    key_width = key_weight.shape[1]
    proj_width = query_width + 2 * key_width
    partial = jnp.concatenate(
        [
            jnp.dot(scaled, query_weight, preferred_element_type=jnp.float32),
            jnp.dot(scaled, key_weight, preferred_element_type=jnp.float32),
            jnp.dot(scaled, value_weight, preferred_element_type=jnp.float32),
        ],
        axis=1,
    )
    arrived = lax.all_to_all(
        partial.reshape(device_count, local_beams, proj_width), "dp", 0, 0, tiled=True
    )
    summed = jnp.sum(arrived, axis=0) * inverse[:, None]

    first_beam = device_rank * local_beams
    my_parent = lax.dynamic_slice_in_dim(parent_beam, first_beam, local_beams)
    my_alive = lax.dynamic_slice_in_dim(beam_alive, first_beam, local_beams)
    position = jnp.take(cache_lengths, my_parent)
    head_count = query_width // HEAD_DIM
    group_count = key_width // HEAD_DIM
    queries = rotate(
        summed[:, :query_width].reshape(local_beams, head_count, HEAD_DIM), position
    ).astype(jnp.bfloat16)
    key_new = rotate(
        summed[:, query_width : query_width + key_width].reshape(
            local_beams, group_count, HEAD_DIM
        ),
        position,
    ).astype(jnp.bfloat16)
    value_new = (
        summed[:, query_width + key_width :]
        .reshape(local_beams, group_count, HEAD_DIM)
        .astype(jnp.bfloat16)
    )
    packed = jnp.concatenate([queries, key_new, value_new], axis=1)
    rows = packed.shape[1]

    source = my_parent // local_beams
    target = source * capacity + arrival_ranks(source)
    slot_of = jnp.arange(slot_total, dtype=jnp.int32)
    match = target[None, :] == slot_of[:, None]
    filled = jnp.any(match, axis=1)
    sender = jnp.argmax(match, axis=1)
    outgoing = jnp.where(
        filled[:, None, None], jnp.take(packed, sender, axis=0), jnp.zeros_like(packed[:1])
    )
    incoming = lax.all_to_all(
        outgoing.reshape(device_count, capacity, rows, HEAD_DIM), "dp", 0, 0, tiled=True
    ).reshape(slot_total, rows, HEAD_DIM)

    all_parents = parent_beam.reshape(device_count, local_beams)
    all_sources = all_parents // local_beams
    destination = jnp.broadcast_to(
        jnp.arange(device_count, dtype=jnp.int32)[:, None], (device_count, local_beams)
    )
    placed = jnp.where(
        all_sources == device_rank, destination * capacity + arrival_ranks(all_sources), slot_total
    )
    local_parent = (
        jnp.zeros((slot_total,), jnp.int32)
        .at[placed.reshape(-1)]
        .set((all_parents % local_beams).reshape(-1), mode="drop")
    )
    slot_length = jnp.take(cache_lengths, first_beam + local_parent)

    cache_rows = key_value_cache.reshape(
        local_beams, key_value_cache.shape[1], 2 * key_value_cache.shape[-1]
    )
    mixed = attend_slots(incoming, cache_rows, local_parent, slot_length)
    returned = lax.all_to_all(
        mixed.reshape(device_count, capacity, head_count * HEAD_DIM), "dp", 0, 0, tiled=True
    ).reshape(slot_total, head_count * HEAD_DIM)
    attention = jnp.take(returned, target, axis=0)
    attention = jnp.where(my_alive[:, None] > 0, attention, jnp.zeros_like(attention))

    spread = jnp.broadcast_to(attention[None], (device_count,) + attention.shape)
    gathered = lax.all_to_all(spread, "dp", 0, 0, tiled=True).reshape(
        device_count * local_beams, head_count * HEAD_DIM
    )
    partial_sum = jnp.dot(gathered, output_weight, preferred_element_type=jnp.float32)
    total_rows, out_width = partial_sum.shape
    reduced = jnp.sum(
        lax.all_to_all(
            partial_sum.reshape(tensor_count, total_rows // tensor_count, out_width),
            "tensor",
            0,
            0,
            tiled=True,
        ),
        axis=0,
    ).astype(jnp.bfloat16)
    copies = jnp.broadcast_to(reduced[None], (tensor_count,) + reduced.shape)
    return lax.all_to_all(copies, "tensor", 0, 0, tiled=True).reshape(total_rows, out_width)


def solution(mesh):
    placed = (
        P("dp", None),
        P("dp"),
        P("dp", "tensor"),
        P("dp", "tensor"),
        P("dp", "tensor"),
        P("tensor", "dp"),
        P("dp", None, None, "tensor", None),
        P(),
        P(),
        P(),
    )
    return jax.shard_map(body, mesh=mesh, in_specs=placed, out_specs=P(None, "dp"), check_vma=False)
```

```python
import functools
import math

import jax
import jax.numpy as jnp
from jax import lax
from jax.experimental import pallas as pl
from jax.experimental.pallas import tpu as pltpu
from jax.sharding import PartitionSpec as P

HEAD_DIM = 128
SLOTS_PER_STEP = 8
PLANE_Y = 4


def rotate(vectors, position):
    half_width = vectors.shape[-1] // 2
    pair_index = jnp.arange(half_width).astype(jnp.float32)
    frequency = jnp.exp(pair_index * (-2.0 * math.log(1000000.0) / vectors.shape[-1]))
    angles = position.astype(jnp.float32)[:, None] * frequency[None, :]
    cosine = jnp.cos(angles)[:, None, :]
    sine_part = jnp.sin(angles)[:, None, :]
    first_half = vectors[..., :half_width]
    second = vectors[..., half_width:]
    return jnp.concatenate(
        [first_half * cosine - second * sine_part, second * cosine + first_half * sine_part],
        axis=-1,
    )


def arrival_ranks(sources):
    ordinal = jnp.arange(sources.shape[-1], dtype=jnp.int32)
    earlier = (sources[..., None, :] == sources[..., :, None]) & (
        ordinal[None, :] < ordinal[:, None]
    )
    return jnp.sum(earlier.astype(jnp.int32), axis=-1)


def attend_kernel(parent_ref, length_ref, packed_ref, *refs):
    cache_refs = refs[:-1]
    out_ref = refs[-1]
    group = len(cache_refs)
    step = pl.program_id(0)
    head_width = packed_ref.shape[-1]
    head_total = packed_ref.shape[1] - 2
    for g in range(group):
        length = length_ref[step * group + g]

        @pl.when(length == 0)
        def _():
            out_ref[g] = jnp.zeros(out_ref.shape[1:], out_ref.dtype)

        @pl.when(length > 0)
        def _():
            attend_one(packed_ref, cache_refs[g], out_ref, g, length, head_total, head_width)


def attend_one(packed_ref, cache_ref, out_ref, g, length, head_total, head_width):
    score_scale = 1.0 / math.sqrt(head_width)
    if True:
        row = packed_ref[g].astype(jnp.float32)
        queries = row[:head_total].astype(jnp.bfloat16)
        key_new = row[head_total : head_total + 1]
        value_new = row[head_total + 1 : head_total + 2]
        block = cache_ref[0]
        keys = block[:, :head_width]
        values = block[:, head_width:]
        cached = (
            lax.dot_general(
                queries, keys, (((1,), (1,)), ((), ())), preferred_element_type=jnp.float32
            )
            * score_scale
        )
        latest = (
            jnp.sum(row[:head_total] * key_new, axis=-1, keepdims=True) * score_scale
        )
        slot = lax.broadcasted_iota(jnp.int32, cached.shape, 1)
        cached = jnp.where(slot < length, cached, -jnp.inf)
        highest = jnp.maximum(jnp.max(cached, axis=-1, keepdims=True), latest)
        cached_exp = jnp.exp(cached - highest)
        latest_exp = jnp.exp(latest - highest)
        denominator = jnp.sum(cached_exp, axis=-1, keepdims=True) + latest_exp
        cached_weight = (cached_exp / denominator).astype(jnp.bfloat16)
        latest_weight = (latest_exp / denominator).astype(jnp.bfloat16)
        mixture = jnp.dot(cached_weight, values, preferred_element_type=jnp.float32)
        mixture = mixture + latest_weight.astype(jnp.float32) * value_new
        out_ref[g] = mixture.astype(out_ref.dtype)


def attend_slots(packed, cache_rows, parents, lengths):
    slot_total, rows, head_width = packed.shape
    head_total = rows - 2
    group = SLOTS_PER_STEP
    cache_len, row_width = cache_rows.shape[1], cache_rows.shape[2]

    def cache_map(g):
        return lambda i, parent_ref, length_ref: (parent_ref[i * group + g], 0, 0)

    grid_spec = pltpu.PrefetchScalarGridSpec(
        num_scalar_prefetch=2,
        grid=(slot_total // group,),
        in_specs=[pl.BlockSpec((group, rows, head_width), lambda i, p, l: (i, 0, 0))]
        + [pl.BlockSpec((1, cache_len, row_width), cache_map(g)) for g in range(group)],
        out_specs=pl.BlockSpec((group, head_total, head_width), lambda i, p, l: (i, 0, 0)),
    )
    return pl.pallas_call(
        attend_kernel,
        grid_spec=grid_spec,
        out_shape=jax.ShapeDtypeStruct((slot_total, head_total, head_width), jnp.bfloat16),
    )(parents, lengths, packed, *([cache_rows] * group))


def ring_reduce_scatter(chunks, position, neighbour, direction):
    size = chunks.shape[0]
    acc = lax.dynamic_index_in_dim(chunks, (position - direction) % size, 0, keepdims=False)
    for step in range(size - 1):
        acc = lax.ppermute(acc, "dp", neighbour)
        acc = acc + lax.dynamic_index_in_dim(
            chunks, (position - direction * (step + 2)) % size, 0, keepdims=False
        )
    return acc


def plane_reduce_scatter(partial, local_beams):
    rows, width = partial.shape
    device_count = rows // local_beams
    y_count = PLANE_Y
    z_count = device_count // y_count
    rank = lax.axis_index("dp")
    y_pos, z_pos = rank // z_count, rank % z_count

    def along_z(step):
        return [(i, (i // z_count) * z_count + (i % z_count + step) % z_count) for i in range(device_count)]

    def along_y(step):
        return [(i, ((i // z_count + step) % y_count) * z_count + i % z_count) for i in range(device_count)]

    blocks = partial.reshape(y_count, z_count, local_beams, width)
    quarter = width // 4
    pieces = []
    for part in range(4):
        own = blocks[..., part * quarter : (part + 1) * quarter]
        direction = 1 if part % 2 == 0 else -1
        if part < 2:
            first = ring_reduce_scatter(
                jnp.swapaxes(own, 0, 1), z_pos, along_z(direction), direction
            )
            pieces.append(ring_reduce_scatter(first, y_pos, along_y(direction), direction))
        else:
            first = ring_reduce_scatter(own, y_pos, along_y(direction), direction)
            pieces.append(ring_reduce_scatter(first, z_pos, along_z(direction), direction))
    return jnp.concatenate(pieces, axis=-1)


def body(
    hidden_in,
    norm_gain,
    query_weight,
    key_weight,
    value_weight,
    output_weight,
    key_value_cache,
    cache_lengths,
    parent_beam,
    beam_alive,
):
    device_count = lax.axis_size("dp")
    device_rank = lax.axis_index("dp")
    tensor_count = lax.axis_size("tensor")
    local_beams = hidden_in.shape[0]
    capacity = max(2, (2 * local_beams + device_count - 1) // device_count)
    slot_total = device_count * capacity

    hidden_float = hidden_in.astype(jnp.float32)
    inverse = lax.rsqrt(jnp.mean(hidden_float * hidden_float, axis=1) + 1e-06)
    blocked = lax.all_to_all(hidden_in, "dp", split_axis=1, concat_axis=0, tiled=True)
    scaled = (blocked.astype(jnp.float32) * norm_gain.astype(jnp.float32)[None, :]).astype(
        jnp.bfloat16
    )
    query_width = query_weight.shape[1]
    key_width = key_weight.shape[1]
    proj_width = query_width + 2 * key_width
    partial = jnp.concatenate(
        [
            jnp.dot(scaled, query_weight, preferred_element_type=jnp.float32),
            jnp.dot(scaled, key_weight, preferred_element_type=jnp.float32),
            jnp.dot(scaled, value_weight, preferred_element_type=jnp.float32),
        ],
        axis=1,
    )
    summed = plane_reduce_scatter(partial, local_beams) * inverse[:, None]

    first_beam = device_rank * local_beams
    my_parent = lax.dynamic_slice_in_dim(parent_beam, first_beam, local_beams)
    my_alive = lax.dynamic_slice_in_dim(beam_alive, first_beam, local_beams)
    position = jnp.take(cache_lengths, my_parent)
    head_count = query_width // HEAD_DIM
    group_count = key_width // HEAD_DIM
    queries = rotate(
        summed[:, :query_width].reshape(local_beams, head_count, HEAD_DIM), position
    ).astype(jnp.bfloat16)
    key_new = rotate(
        summed[:, query_width : query_width + key_width].reshape(
            local_beams, group_count, HEAD_DIM
        ),
        position,
    ).astype(jnp.bfloat16)
    value_new = (
        summed[:, query_width + key_width :]
        .reshape(local_beams, group_count, HEAD_DIM)
        .astype(jnp.bfloat16)
    )
    packed = jnp.concatenate([queries, key_new, value_new], axis=1)
    rows = packed.shape[1]

    source = my_parent // local_beams
    target = source * capacity + arrival_ranks(source)
    slot_of = jnp.arange(slot_total, dtype=jnp.int32)
    match = target[None, :] == slot_of[:, None]
    filled = jnp.any(match, axis=1)
    sender = jnp.argmax(match, axis=1)
    outgoing = jnp.where(
        filled[:, None, None], jnp.take(packed, sender, axis=0), jnp.zeros_like(packed[:1])
    )
    incoming = lax.all_to_all(
        outgoing.reshape(device_count, capacity, rows, HEAD_DIM), "dp", 0, 0, tiled=True
    ).reshape(slot_total, rows, HEAD_DIM)

    all_parents = parent_beam.reshape(device_count, local_beams)
    all_sources = all_parents // local_beams
    destination = jnp.broadcast_to(
        jnp.arange(device_count, dtype=jnp.int32)[:, None], (device_count, local_beams)
    )
    placed = jnp.where(
        all_sources == device_rank, destination * capacity + arrival_ranks(all_sources), slot_total
    )
    local_parent = (
        jnp.zeros((slot_total,), jnp.int32)
        .at[placed.reshape(-1)]
        .set((all_parents % local_beams).reshape(-1), mode="drop")
    )
    used = jnp.zeros((slot_total,), jnp.int32).at[placed.reshape(-1)].set(1, mode="drop")
    slot_length = jnp.take(cache_lengths, first_beam + local_parent) * used

    cache_rows = key_value_cache.reshape(
        local_beams, key_value_cache.shape[1], 2 * key_value_cache.shape[-1]
    )
    mixed = attend_slots(incoming, cache_rows, local_parent, slot_length)
    returned = lax.all_to_all(
        mixed.reshape(device_count, capacity, head_count * HEAD_DIM), "dp", 0, 0, tiled=True
    ).reshape(slot_total, head_count * HEAD_DIM)
    attention = jnp.take(returned, target, axis=0)
    attention = jnp.where(my_alive[:, None] > 0, attention, jnp.zeros_like(attention))

    spread = jnp.broadcast_to(attention[None], (device_count,) + attention.shape)
    gathered = lax.all_to_all(spread, "dp", 0, 0, tiled=True).reshape(
        device_count * local_beams, head_count * HEAD_DIM
    )
    partial_sum = jnp.dot(gathered, output_weight, preferred_element_type=jnp.float32)
    total_rows, out_width = partial_sum.shape
    reduced = jnp.sum(
        lax.all_to_all(
            partial_sum.reshape(tensor_count, total_rows // tensor_count, out_width),
            "tensor",
            0,
            0,
            tiled=True,
        ),
        axis=0,
    ).astype(jnp.bfloat16)
    copies = jnp.broadcast_to(reduced[None], (tensor_count,) + reduced.shape)
    return lax.all_to_all(copies, "tensor", 0, 0, tiled=True).reshape(total_rows, out_width)


def solution(mesh):
    placed = (
        P("dp", None),
        P("dp"),
        P("dp", "tensor"),
        P("dp", "tensor"),
        P("dp", "tensor"),
        P("tensor", "dp"),
        P("dp", None, None, "tensor", None),
        P(),
        P(),
        P(),
    )
    return jax.shard_map(body, mesh=mesh, in_specs=placed, out_specs=P(None, "dp"), check_vma=False)
```

```python
import functools
import math

import jax
import jax.numpy as jnp
from jax import lax
from jax.experimental import pallas as pl
from jax.experimental.pallas import tpu as pltpu
from jax.sharding import PartitionSpec as P

HEAD_DIM = 128
SLOTS_PER_STEP = 8


def rotate(vectors, position):
    half_width = vectors.shape[-1] // 2
    pair_index = jnp.arange(half_width).astype(jnp.float32)
    frequency = jnp.exp(pair_index * (-2.0 * math.log(1000000.0) / vectors.shape[-1]))
    angles = position.astype(jnp.float32)[:, None] * frequency[None, :]
    cosine = jnp.cos(angles)[:, None, :]
    sine_part = jnp.sin(angles)[:, None, :]
    first_half = vectors[..., :half_width]
    second = vectors[..., half_width:]
    return jnp.concatenate(
        [first_half * cosine - second * sine_part, second * cosine + first_half * sine_part],
        axis=-1,
    )


def arrival_ranks(sources):
    ordinal = jnp.arange(sources.shape[-1], dtype=jnp.int32)
    earlier = (sources[..., None, :] == sources[..., :, None]) & (
        ordinal[None, :] < ordinal[:, None]
    )
    return jnp.sum(earlier.astype(jnp.int32), axis=-1)


def attend_kernel(parent_ref, length_ref, packed_ref, *refs):
    cache_refs = refs[:-1]
    out_ref = refs[-1]
    group = len(cache_refs)
    step = pl.program_id(0)
    head_width = packed_ref.shape[-1]
    head_total = packed_ref.shape[1] - 2
    for g in range(group):
        length = length_ref[step * group + g]

        @pl.when(length == 0)
        def _():
            out_ref[g] = jnp.zeros(out_ref.shape[1:], out_ref.dtype)

        @pl.when(length > 0)
        def _():
            attend_one(packed_ref, cache_refs[g], out_ref, g, length, head_total, head_width)


def attend_one(packed_ref, cache_ref, out_ref, g, length, head_total, head_width):
    score_scale = 1.0 / math.sqrt(head_width)
    if True:
        row = packed_ref[g].astype(jnp.float32)
        queries = row[:head_total].astype(jnp.bfloat16)
        key_new = row[head_total : head_total + 1]
        value_new = row[head_total + 1 : head_total + 2]
        block = cache_ref[0]
        keys = block[:, :head_width]
        values = block[:, head_width:]
        cached = (
            lax.dot_general(
                queries, keys, (((1,), (1,)), ((), ())), preferred_element_type=jnp.float32
            )
            * score_scale
        )
        latest = (
            jnp.sum(row[:head_total] * key_new, axis=-1, keepdims=True) * score_scale
        )
        slot = lax.broadcasted_iota(jnp.int32, cached.shape, 1)
        cached = jnp.where(slot < length, cached, -jnp.inf)
        highest = jnp.maximum(jnp.max(cached, axis=-1, keepdims=True), latest)
        cached_exp = jnp.exp(cached - highest)
        latest_exp = jnp.exp(latest - highest)
        denominator = jnp.sum(cached_exp, axis=-1, keepdims=True) + latest_exp
        cached_weight = (cached_exp / denominator).astype(jnp.bfloat16)
        latest_weight = (latest_exp / denominator).astype(jnp.bfloat16)
        mixture = jnp.dot(cached_weight, values, preferred_element_type=jnp.float32)
        mixture = mixture + latest_weight.astype(jnp.float32) * value_new
        out_ref[g] = mixture.astype(out_ref.dtype)


def attend_slots(packed, cache_rows, parents, lengths):
    slot_total, rows, head_width = packed.shape
    head_total = rows - 2
    group = SLOTS_PER_STEP
    cache_len, row_width = cache_rows.shape[1], cache_rows.shape[2]

    def cache_map(g):
        return lambda i, parent_ref, length_ref: (parent_ref[i * group + g], 0, 0)

    grid_spec = pltpu.PrefetchScalarGridSpec(
        num_scalar_prefetch=2,
        grid=(slot_total // group,),
        in_specs=[pl.BlockSpec((group, rows, head_width), lambda i, p, l: (i, 0, 0))]
        + [pl.BlockSpec((1, cache_len, row_width), cache_map(g)) for g in range(group)],
        out_specs=pl.BlockSpec((group, head_total, head_width), lambda i, p, l: (i, 0, 0)),
    )
    return pl.pallas_call(
        attend_kernel,
        grid_spec=grid_spec,
        out_shape=jax.ShapeDtypeStruct((slot_total, head_total, head_width), jnp.bfloat16),
    )(parents, lengths, packed, *([cache_rows] * group))


def body(
    hidden_in,
    norm_gain,
    query_weight,
    key_weight,
    value_weight,
    output_weight,
    key_value_cache,
    cache_lengths,
    parent_beam,
    beam_alive,
):
    device_count = lax.axis_size("dp")
    device_rank = lax.axis_index("dp")
    tensor_count = lax.axis_size("tensor")
    local_beams = hidden_in.shape[0]
    capacity = max(2, (2 * local_beams + device_count - 1) // device_count)
    slot_total = device_count * capacity

    hidden_float = hidden_in.astype(jnp.float32)
    inverse = lax.rsqrt(jnp.mean(hidden_float * hidden_float, axis=1) + 1e-06)

    features = query_weight.shape[0]
    pair_count = device_count // 2
    is_low = device_rank % 2 == 0
    partner = [(i, i ^ 1) for i in range(device_count)]
    query_width = query_weight.shape[1]
    key_width = key_weight.shape[1]
    query_half = query_width // 2
    key_half = key_width // 2
    low_cols = jnp.concatenate(
        [query_weight[:, :query_half], key_weight[:, :key_half], value_weight[:, :key_half]],
        axis=1,
    )
    high_cols = jnp.concatenate(
        [query_weight[:, query_half:], key_weight[:, key_half:], value_weight[:, key_half:]],
        axis=1,
    )
    mine = jnp.where(is_low, low_cols, high_cols)
    received = lax.ppermute(jnp.where(is_low, high_cols, low_cols), "dp", partner)
    partner_gain = lax.ppermute(norm_gain, "dp", partner)
    pair_weight = jnp.where(
        is_low, jnp.concatenate([mine, received], 0), jnp.concatenate([received, mine], 0)
    )
    pair_gain = jnp.where(
        is_low,
        jnp.concatenate([norm_gain, partner_gain]),
        jnp.concatenate([partner_gain, norm_gain]),
    )
    spread = jnp.swapaxes(
        jnp.repeat(hidden_in.reshape(local_beams, pair_count, 2 * features), 2, axis=1), 0, 1
    )
    blocked = lax.all_to_all(spread, "dp", 0, 0, tiled=True).reshape(
        device_count * local_beams, 2 * features
    )
    scaled = (blocked.astype(jnp.float32) * pair_gain.astype(jnp.float32)[None, :]).astype(
        jnp.bfloat16
    )
    partial = jnp.dot(scaled, pair_weight, preferred_element_type=jnp.float32)
    half_width = partial.shape[1]
    arrived = lax.all_to_all(
        partial.reshape(device_count, local_beams, half_width), "dp", 0, 0, tiled=True
    )
    sums = jnp.sum(arrived.reshape(pair_count, 2, local_beams, half_width), axis=0)
    key_end = query_half + key_half
    summed = jnp.concatenate(
        [
            sums[0, :, :query_half],
            sums[1, :, :query_half],
            sums[0, :, query_half:key_end],
            sums[1, :, query_half:key_end],
            sums[0, :, key_end:],
            sums[1, :, key_end:],
        ],
        axis=1,
    ) * inverse[:, None]
    cache_rows = key_value_cache.reshape(
        local_beams, key_value_cache.shape[1], 2 * key_value_cache.shape[-1]
    )
    summed, cache_rows = lax.optimization_barrier((summed, cache_rows))

    first_beam = device_rank * local_beams
    my_parent = lax.dynamic_slice_in_dim(parent_beam, first_beam, local_beams)
    my_alive = lax.dynamic_slice_in_dim(beam_alive, first_beam, local_beams)
    position = jnp.take(cache_lengths, my_parent)
    head_count = query_width // HEAD_DIM
    group_count = key_width // HEAD_DIM
    queries = rotate(
        summed[:, :query_width].reshape(local_beams, head_count, HEAD_DIM), position
    ).astype(jnp.bfloat16)
    key_new = rotate(
        summed[:, query_width : query_width + key_width].reshape(
            local_beams, group_count, HEAD_DIM
        ),
        position,
    ).astype(jnp.bfloat16)
    value_new = (
        summed[:, query_width + key_width :]
        .reshape(local_beams, group_count, HEAD_DIM)
        .astype(jnp.bfloat16)
    )
    packed = jnp.concatenate([queries, key_new, value_new], axis=1)
    rows = packed.shape[1]

    source = my_parent // local_beams
    target = source * capacity + arrival_ranks(source)
    slot_of = jnp.arange(slot_total, dtype=jnp.int32)
    match = target[None, :] == slot_of[:, None]
    filled = jnp.any(match, axis=1)
    sender = jnp.argmax(match, axis=1)
    outgoing = jnp.where(
        filled[:, None, None], jnp.take(packed, sender, axis=0), jnp.zeros_like(packed[:1])
    )
    incoming = lax.all_to_all(
        outgoing.reshape(device_count, capacity, rows, HEAD_DIM), "dp", 0, 0, tiled=True
    ).reshape(slot_total, rows, HEAD_DIM)

    all_parents = parent_beam.reshape(device_count, local_beams)
    all_sources = all_parents // local_beams
    destination = jnp.broadcast_to(
        jnp.arange(device_count, dtype=jnp.int32)[:, None], (device_count, local_beams)
    )
    placed = jnp.where(
        all_sources == device_rank, destination * capacity + arrival_ranks(all_sources), slot_total
    )
    chosen = placed.reshape(-1)[None, :] == slot_of[:, None]
    local_parent = jnp.sum(
        jnp.where(chosen, (all_parents % local_beams).reshape(-1)[None, :], 0), axis=1
    )
    used = jnp.any(chosen, axis=1).astype(jnp.int32)
    slot_length = jnp.take(cache_lengths, first_beam + local_parent) * used

    mixed = attend_slots(incoming, cache_rows, local_parent, slot_length)
    returned = lax.all_to_all(
        mixed.reshape(device_count, capacity, head_count * HEAD_DIM), "dp", 0, 0, tiled=True
    ).reshape(slot_total, head_count * HEAD_DIM)
    attention = jnp.take(returned, target, axis=0)
    attention = jnp.where(my_alive[:, None] > 0, attention, jnp.zeros_like(attention))

    spread = jnp.broadcast_to(attention[None], (device_count,) + attention.shape)
    gathered = lax.all_to_all(spread, "dp", 0, 0, tiled=True).reshape(
        device_count * local_beams, head_count * HEAD_DIM
    )
    partial_sum = jnp.dot(gathered, output_weight, preferred_element_type=jnp.float32)
    total_rows, out_width = partial_sum.shape
    reduced = jnp.sum(
        lax.all_to_all(
            partial_sum.reshape(tensor_count, total_rows // tensor_count, out_width),
            "tensor",
            0,
            0,
            tiled=True,
        ),
        axis=0,
    ).astype(jnp.bfloat16)
    copies = jnp.broadcast_to(reduced[None], (tensor_count,) + reduced.shape)
    return lax.all_to_all(copies, "tensor", 0, 0, tiled=True).reshape(total_rows, out_width)


def solution(mesh):
    placed = (
        P("dp", None),
        P("dp"),
        P("dp", "tensor"),
        P("dp", "tensor"),
        P("dp", "tensor"),
        P("tensor", "dp"),
        P("dp", None, None, "tensor", None),
        P(),
        P(),
        P(),
    )
    return jax.shard_map(body, mesh=mesh, in_specs=placed, out_specs=P(None, "dp"), check_vma=False)
```

```python
import functools
import math

import jax
import jax.numpy as jnp
from jax import lax
from jax.experimental import pallas as pl
from jax.experimental.pallas import tpu as pltpu
from jax.sharding import PartitionSpec as P

HEAD_DIM = 128
SLOTS_PER_STEP = 8


def rotate(vectors, position):
    half_width = vectors.shape[-1] // 2
    pair_index = jnp.arange(half_width).astype(jnp.float32)
    frequency = jnp.exp(pair_index * (-2.0 * math.log(1000000.0) / vectors.shape[-1]))
    angles = position.astype(jnp.float32)[:, None] * frequency[None, :]
    cosine = jnp.cos(angles)[:, None, :]
    sine_part = jnp.sin(angles)[:, None, :]
    first_half = vectors[..., :half_width]
    second = vectors[..., half_width:]
    return jnp.concatenate(
        [first_half * cosine - second * sine_part, second * cosine + first_half * sine_part],
        axis=-1,
    )


def arrival_ranks(sources):
    ordinal = jnp.arange(sources.shape[-1], dtype=jnp.int32)
    earlier = (sources[..., None, :] == sources[..., :, None]) & (
        ordinal[None, :] < ordinal[:, None]
    )
    return jnp.sum(earlier.astype(jnp.int32), axis=-1)


def attend_kernel(parent_ref, length_ref, packed_ref, *refs):
    cache_refs = refs[:-1]
    out_ref = refs[-1]
    group = len(cache_refs)
    step = pl.program_id(0)
    head_width = packed_ref.shape[-1]
    head_total = packed_ref.shape[1] - 2
    for g in range(group):
        length = length_ref[step * group + g]

        @pl.when(length == 0)
        def _():
            out_ref[g] = jnp.zeros(out_ref.shape[1:], out_ref.dtype)

        @pl.when(length > 0)
        def _():
            attend_one(packed_ref, cache_refs[g], out_ref, g, length, head_total, head_width)


def attend_one(packed_ref, cache_ref, out_ref, g, length, head_total, head_width):
    score_scale = 1.0 / math.sqrt(head_width)
    if True:
        row = packed_ref[g].astype(jnp.float32)
        queries = row[:head_total].astype(jnp.bfloat16)
        key_new = row[head_total : head_total + 1]
        value_new = row[head_total + 1 : head_total + 2]
        block = cache_ref[0]
        keys = block[:, :head_width]
        values = block[:, head_width:]
        cached = (
            lax.dot_general(
                queries, keys, (((1,), (1,)), ((), ())), preferred_element_type=jnp.float32
            )
            * score_scale
        )
        latest = (
            jnp.sum(row[:head_total] * key_new, axis=-1, keepdims=True) * score_scale
        )
        slot = lax.broadcasted_iota(jnp.int32, cached.shape, 1)
        cached = jnp.where(slot < length, cached, -jnp.inf)
        highest = jnp.maximum(jnp.max(cached, axis=-1, keepdims=True), latest)
        cached_exp = jnp.exp(cached - highest)
        latest_exp = jnp.exp(latest - highest)
        denominator = jnp.sum(cached_exp, axis=-1, keepdims=True) + latest_exp
        cached_weight = (cached_exp / denominator).astype(jnp.bfloat16)
        latest_weight = (latest_exp / denominator).astype(jnp.bfloat16)
        mixture = jnp.dot(cached_weight, values, preferred_element_type=jnp.float32)
        mixture = mixture + latest_weight.astype(jnp.float32) * value_new
        out_ref[g] = mixture.astype(out_ref.dtype)


def attend_slots(packed, cache_rows, parents, lengths):
    slot_total, rows, head_width = packed.shape
    head_total = rows - 2
    group = SLOTS_PER_STEP
    cache_len, row_width = cache_rows.shape[1], cache_rows.shape[2]

    def cache_map(g):
        return lambda i, parent_ref, length_ref: (parent_ref[i * group + g], 0, 0)

    grid_spec = pltpu.PrefetchScalarGridSpec(
        num_scalar_prefetch=2,
        grid=(slot_total // group,),
        in_specs=[pl.BlockSpec((group, rows, head_width), lambda i, p, l: (i, 0, 0))]
        + [pl.BlockSpec((1, cache_len, row_width), cache_map(g)) for g in range(group)],
        out_specs=pl.BlockSpec((group, head_total, head_width), lambda i, p, l: (i, 0, 0)),
    )
    return pl.pallas_call(
        attend_kernel,
        grid_spec=grid_spec,
        out_shape=jax.ShapeDtypeStruct((slot_total, head_total, head_width), jnp.bfloat16),
    )(parents, lengths, packed, *([cache_rows] * group))


def body(
    hidden_in,
    norm_gain,
    query_weight,
    key_weight,
    value_weight,
    output_weight,
    key_value_cache,
    cache_lengths,
    parent_beam,
    beam_alive,
):
    device_count = lax.axis_size("dp")
    device_rank = lax.axis_index("dp")
    tensor_count = lax.axis_size("tensor")
    local_beams = hidden_in.shape[0]
    capacity = max(2, (2 * local_beams + device_count - 1) // device_count)
    slot_total = device_count * capacity

    hidden_float = hidden_in.astype(jnp.float32)
    inverse = lax.rsqrt(jnp.mean(hidden_float * hidden_float, axis=1) + 1e-06)

    features = query_weight.shape[0]
    pair_count = device_count // 2
    is_low = device_rank % 2 == 0
    partner = [(i, i ^ 1) for i in range(device_count)]
    query_width = query_weight.shape[1]
    key_width = key_weight.shape[1]
    query_half = query_width // 2
    key_half = key_width // 2
    low_cols = jnp.concatenate(
        [query_weight[:, :query_half], key_weight[:, :key_half], value_weight[:, :key_half]],
        axis=1,
    )
    high_cols = jnp.concatenate(
        [query_weight[:, query_half:], key_weight[:, key_half:], value_weight[:, key_half:]],
        axis=1,
    )
    mine = jnp.where(is_low, low_cols, high_cols)
    received = lax.ppermute(jnp.where(is_low, high_cols, low_cols), "dp", partner)
    partner_gain = lax.ppermute(norm_gain, "dp", partner)
    pair_weight = jnp.where(
        is_low, jnp.concatenate([mine, received], 0), jnp.concatenate([received, mine], 0)
    )
    pair_gain = jnp.where(
        is_low,
        jnp.concatenate([norm_gain, partner_gain]),
        jnp.concatenate([partner_gain, norm_gain]),
    )
    spread = jnp.swapaxes(
        jnp.repeat(hidden_in.reshape(local_beams, pair_count, 2 * features), 2, axis=1), 0, 1
    )
    blocked = lax.all_to_all(spread, "dp", 0, 0, tiled=True).reshape(
        device_count * local_beams, 2 * features
    )
    scaled = (blocked.astype(jnp.float32) * pair_gain.astype(jnp.float32)[None, :]).astype(
        jnp.bfloat16
    )
    partial = jnp.dot(scaled, pair_weight, preferred_element_type=jnp.float32)
    half_width = partial.shape[1]
    arrived = lax.all_to_all(
        partial.astype(jnp.bfloat16).reshape(device_count, local_beams, half_width),
        "dp",
        0,
        0,
        tiled=True,
    )
    sums = jnp.sum(
        arrived.astype(jnp.float32).reshape(pair_count, 2, local_beams, half_width), axis=0
    )
    key_end = query_half + key_half
    summed = jnp.concatenate(
        [
            sums[0, :, :query_half],
            sums[1, :, :query_half],
            sums[0, :, query_half:key_end],
            sums[1, :, query_half:key_end],
            sums[0, :, key_end:],
            sums[1, :, key_end:],
        ],
        axis=1,
    ) * inverse[:, None]
    cache_rows = key_value_cache.reshape(
        local_beams, key_value_cache.shape[1], 2 * key_value_cache.shape[-1]
    )
    summed, cache_rows = lax.optimization_barrier((summed, cache_rows))

    first_beam = device_rank * local_beams
    my_parent = lax.dynamic_slice_in_dim(parent_beam, first_beam, local_beams)
    my_alive = lax.dynamic_slice_in_dim(beam_alive, first_beam, local_beams)
    position = jnp.take(cache_lengths, my_parent)
    head_count = query_width // HEAD_DIM
    group_count = key_width // HEAD_DIM
    queries = rotate(
        summed[:, :query_width].reshape(local_beams, head_count, HEAD_DIM), position
    ).astype(jnp.bfloat16)
    key_new = rotate(
        summed[:, query_width : query_width + key_width].reshape(
            local_beams, group_count, HEAD_DIM
        ),
        position,
    ).astype(jnp.bfloat16)
    value_new = (
        summed[:, query_width + key_width :]
        .reshape(local_beams, group_count, HEAD_DIM)
        .astype(jnp.bfloat16)
    )
    packed = jnp.concatenate([queries, key_new, value_new], axis=1)
    rows = packed.shape[1]

    source = my_parent // local_beams
    target = source * capacity + arrival_ranks(source)
    slot_of = jnp.arange(slot_total, dtype=jnp.int32)
    match = target[None, :] == slot_of[:, None]
    filled = jnp.any(match, axis=1)
    sender = jnp.argmax(match, axis=1)
    outgoing = jnp.where(
        filled[:, None, None], jnp.take(packed, sender, axis=0), jnp.zeros_like(packed[:1])
    )
    incoming = lax.all_to_all(
        outgoing.reshape(device_count, capacity, rows, HEAD_DIM), "dp", 0, 0, tiled=True
    ).reshape(slot_total, rows, HEAD_DIM)

    all_parents = parent_beam.reshape(device_count, local_beams)
    all_sources = all_parents // local_beams
    destination = jnp.broadcast_to(
        jnp.arange(device_count, dtype=jnp.int32)[:, None], (device_count, local_beams)
    )
    placed = jnp.where(
        all_sources == device_rank, destination * capacity + arrival_ranks(all_sources), slot_total
    )
    chosen = placed.reshape(-1)[None, :] == slot_of[:, None]
    local_parent = jnp.sum(
        jnp.where(chosen, (all_parents % local_beams).reshape(-1)[None, :], 0), axis=1
    )
    used = jnp.any(chosen, axis=1).astype(jnp.int32)
    slot_length = jnp.take(cache_lengths, first_beam + local_parent) * used

    mixed = attend_slots(incoming, cache_rows, local_parent, slot_length)
    returned = lax.all_to_all(
        mixed.reshape(device_count, capacity, head_count * HEAD_DIM), "dp", 0, 0, tiled=True
    ).reshape(slot_total, head_count * HEAD_DIM)
    attention = jnp.take(returned, target, axis=0)
    attention = jnp.where(my_alive[:, None] > 0, attention, jnp.zeros_like(attention))

    spread = jnp.broadcast_to(attention[None], (device_count,) + attention.shape)
    gathered = lax.all_to_all(spread, "dp", 0, 0, tiled=True).reshape(
        device_count * local_beams, head_count * HEAD_DIM
    )
    partial_sum = jnp.dot(gathered, output_weight, preferred_element_type=jnp.float32)
    total_rows, out_width = partial_sum.shape
    reduced = jnp.sum(
        lax.all_to_all(
            partial_sum.reshape(tensor_count, total_rows // tensor_count, out_width),
            "tensor",
            0,
            0,
            tiled=True,
        ),
        axis=0,
    ).astype(jnp.bfloat16)
    copies = jnp.broadcast_to(reduced[None], (tensor_count,) + reduced.shape)
    return lax.all_to_all(copies, "tensor", 0, 0, tiled=True).reshape(total_rows, out_width)


def solution(mesh):
    placed = (
        P("dp", None),
        P("dp"),
        P("dp", "tensor"),
        P("dp", "tensor"),
        P("dp", "tensor"),
        P("tensor", "dp"),
        P("dp", None, None, "tensor", None),
        P(),
        P(),
        P(),
    )
    return jax.shard_map(body, mesh=mesh, in_specs=placed, out_specs=P(None, "dp"), check_vma=False)
```

```python
import functools
import math

import jax
import jax.numpy as jnp
from jax import lax
from jax.experimental import pallas as pl
from jax.experimental.pallas import tpu as pltpu
from jax.sharding import PartitionSpec as P

HEAD_DIM = 128
SLOTS_PER_STEP = 8
PLANE_Y = 4
DP = ("dy", "dz")
TP = ("tx", "tc")


def rotate(vectors, position):
    half_width = vectors.shape[-1] // 2
    pair_index = jnp.arange(half_width).astype(jnp.float32)
    frequency = jnp.exp(pair_index * (-2.0 * math.log(1000000.0) / vectors.shape[-1]))
    angles = position.astype(jnp.float32)[:, None] * frequency[None, :]
    cosine = jnp.cos(angles)[:, None, :]
    sine_part = jnp.sin(angles)[:, None, :]
    first_half = vectors[..., :half_width]
    second = vectors[..., half_width:]
    return jnp.concatenate(
        [first_half * cosine - second * sine_part, second * cosine + first_half * sine_part],
        axis=-1,
    )


def arrival_ranks(sources):
    ordinal = jnp.arange(sources.shape[-1], dtype=jnp.int32)
    earlier = (sources[..., None, :] == sources[..., :, None]) & (
        ordinal[None, :] < ordinal[:, None]
    )
    return jnp.sum(earlier.astype(jnp.int32), axis=-1)


def attend_kernel(parent_ref, length_ref, packed_ref, *refs):
    cache_refs = refs[:-1]
    out_ref = refs[-1]
    group = len(cache_refs)
    step = pl.program_id(0)
    head_width = packed_ref.shape[-1]
    head_total = packed_ref.shape[1] - 2
    for g in range(group):
        length = length_ref[step * group + g]

        @pl.when(length == 0)
        def _():
            out_ref[g] = jnp.zeros(out_ref.shape[1:], out_ref.dtype)

        @pl.when(length > 0)
        def _():
            attend_one(packed_ref, cache_refs[g], out_ref, g, length, head_total, head_width)


def attend_one(packed_ref, cache_ref, out_ref, g, length, head_total, head_width):
    score_scale = 1.0 / math.sqrt(head_width)
    if True:
        row = packed_ref[g].astype(jnp.float32)
        queries = row[:head_total].astype(jnp.bfloat16)
        key_new = row[head_total : head_total + 1]
        value_new = row[head_total + 1 : head_total + 2]
        block = cache_ref[0]
        keys = block[:, :head_width]
        values = block[:, head_width:]
        cached = (
            lax.dot_general(
                queries, keys, (((1,), (1,)), ((), ())), preferred_element_type=jnp.float32
            )
            * score_scale
        )
        latest = (
            jnp.sum(row[:head_total] * key_new, axis=-1, keepdims=True) * score_scale
        )
        slot = lax.broadcasted_iota(jnp.int32, cached.shape, 1)
        cached = jnp.where(slot < length, cached, -jnp.inf)
        highest = jnp.maximum(jnp.max(cached, axis=-1, keepdims=True), latest)
        cached_exp = jnp.exp(cached - highest)
        latest_exp = jnp.exp(latest - highest)
        denominator = jnp.sum(cached_exp, axis=-1, keepdims=True) + latest_exp
        cached_weight = (cached_exp / denominator).astype(jnp.bfloat16)
        latest_weight = (latest_exp / denominator).astype(jnp.bfloat16)
        mixture = jnp.dot(cached_weight, values, preferred_element_type=jnp.float32)
        mixture = mixture + latest_weight.astype(jnp.float32) * value_new
        out_ref[g] = mixture.astype(out_ref.dtype)


def attend_slots(packed, cache_rows, parents, lengths):
    slot_total, rows, head_width = packed.shape
    head_total = rows - 2
    group = SLOTS_PER_STEP
    cache_len, row_width = cache_rows.shape[1], cache_rows.shape[2]

    def cache_map(g):
        return lambda i, parent_ref, length_ref: (parent_ref[i * group + g], 0, 0)

    grid_spec = pltpu.PrefetchScalarGridSpec(
        num_scalar_prefetch=2,
        grid=(slot_total // group,),
        in_specs=[pl.BlockSpec((group, rows, head_width), lambda i, p, l: (i, 0, 0))]
        + [pl.BlockSpec((1, cache_len, row_width), cache_map(g)) for g in range(group)],
        out_specs=pl.BlockSpec((group, head_total, head_width), lambda i, p, l: (i, 0, 0)),
    )
    return pl.pallas_call(
        attend_kernel,
        grid_spec=grid_spec,
        out_shape=jax.ShapeDtypeStruct((slot_total, head_total, head_width), jnp.bfloat16),
    )(parents, lengths, packed, *([cache_rows] * group))


def body(
    hidden_in,
    norm_gain,
    query_weight,
    key_weight,
    value_weight,
    output_weight,
    key_value_cache,
    cache_lengths,
    parent_beam,
    beam_alive,
):
    device_count = lax.axis_size(DP)
    device_rank = lax.axis_index(DP)
    local_beams = hidden_in.shape[0]
    capacity = max(2, (2 * local_beams + device_count - 1) // device_count)
    slot_total = device_count * capacity

    hidden_float = hidden_in.astype(jnp.float32)
    inverse = lax.rsqrt(jnp.mean(hidden_float * hidden_float, axis=1) + 1e-06)

    features = query_weight.shape[0]
    pair_count = device_count // 2
    is_low = device_rank % 2 == 0
    partner = [(i, i ^ 1) for i in range(device_count)]
    query_width = query_weight.shape[1]
    key_width = key_weight.shape[1]
    query_half = query_width // 2
    key_half = key_width // 2
    low_cols = jnp.concatenate(
        [query_weight[:, :query_half], key_weight[:, :key_half], value_weight[:, :key_half]],
        axis=1,
    )
    high_cols = jnp.concatenate(
        [query_weight[:, query_half:], key_weight[:, key_half:], value_weight[:, key_half:]],
        axis=1,
    )
    mine = jnp.where(is_low, low_cols, high_cols)
    received = lax.ppermute(jnp.where(is_low, high_cols, low_cols), DP, partner)
    partner_gain = lax.ppermute(norm_gain, DP, partner)
    pair_weight = jnp.where(
        is_low, jnp.concatenate([mine, received], 0), jnp.concatenate([received, mine], 0)
    )
    pair_gain = jnp.where(
        is_low,
        jnp.concatenate([norm_gain, partner_gain]),
        jnp.concatenate([partner_gain, norm_gain]),
    )
    spread = jnp.swapaxes(
        jnp.repeat(hidden_in.reshape(local_beams, pair_count, 2 * features), 2, axis=1), 0, 1
    )
    blocked = lax.all_to_all(spread, DP, 0, 0, tiled=True).reshape(
        device_count * local_beams, 2 * features
    )
    scaled = (blocked.astype(jnp.float32) * pair_gain.astype(jnp.float32)[None, :]).astype(
        jnp.bfloat16
    )
    partial = jnp.dot(scaled, pair_weight, preferred_element_type=jnp.float32)
    half_width = partial.shape[1]
    arrived = lax.all_to_all(
        partial.astype(jnp.bfloat16).reshape(device_count, local_beams, half_width),
        DP,
        0,
        0,
        tiled=True,
    )
    sums = jnp.sum(
        arrived.astype(jnp.float32).reshape(pair_count, 2, local_beams, half_width), axis=0
    )
    key_end = query_half + key_half
    summed = jnp.concatenate(
        [
            sums[0, :, :query_half],
            sums[1, :, :query_half],
            sums[0, :, query_half:key_end],
            sums[1, :, query_half:key_end],
            sums[0, :, key_end:],
            sums[1, :, key_end:],
        ],
        axis=1,
    ) * inverse[:, None]
    cache_rows = key_value_cache.reshape(
        local_beams, key_value_cache.shape[1], 2 * key_value_cache.shape[-1]
    )
    summed, cache_rows = lax.optimization_barrier((summed, cache_rows))

    first_beam = device_rank * local_beams
    my_parent = lax.dynamic_slice_in_dim(parent_beam, first_beam, local_beams)
    my_alive = lax.dynamic_slice_in_dim(beam_alive, first_beam, local_beams)
    position = jnp.take(cache_lengths, my_parent)
    head_count = query_width // HEAD_DIM
    group_count = key_width // HEAD_DIM
    queries = rotate(
        summed[:, :query_width].reshape(local_beams, head_count, HEAD_DIM), position
    ).astype(jnp.bfloat16)
    key_new = rotate(
        summed[:, query_width : query_width + key_width].reshape(
            local_beams, group_count, HEAD_DIM
        ),
        position,
    ).astype(jnp.bfloat16)
    value_new = (
        summed[:, query_width + key_width :]
        .reshape(local_beams, group_count, HEAD_DIM)
        .astype(jnp.bfloat16)
    )
    packed = jnp.concatenate([queries, key_new, value_new], axis=1)
    rows = packed.shape[1]

    source = my_parent // local_beams
    target = source * capacity + arrival_ranks(source)
    slot_of = jnp.arange(slot_total, dtype=jnp.int32)
    match = target[None, :] == slot_of[:, None]
    filled = jnp.any(match, axis=1)
    sender = jnp.argmax(match, axis=1)
    outgoing = jnp.where(
        filled[:, None, None], jnp.take(packed, sender, axis=0), jnp.zeros_like(packed[:1])
    )
    incoming = lax.all_to_all(
        outgoing.reshape(device_count, capacity, rows, HEAD_DIM), DP, 0, 0, tiled=True
    ).reshape(slot_total, rows, HEAD_DIM)

    all_parents = parent_beam.reshape(device_count, local_beams)
    all_sources = all_parents // local_beams
    destination = jnp.broadcast_to(
        jnp.arange(device_count, dtype=jnp.int32)[:, None], (device_count, local_beams)
    )
    placed = jnp.where(
        all_sources == device_rank, destination * capacity + arrival_ranks(all_sources), slot_total
    )
    chosen = placed.reshape(-1)[None, :] == slot_of[:, None]
    local_parent = jnp.sum(
        jnp.where(chosen, (all_parents % local_beams).reshape(-1)[None, :], 0), axis=1
    )
    used = jnp.any(chosen, axis=1).astype(jnp.int32)
    slot_length = jnp.take(cache_lengths, first_beam + local_parent) * used

    mixed = attend_slots(incoming, cache_rows, local_parent, slot_length)
    returned = lax.all_to_all(
        mixed.reshape(device_count, capacity, head_count * HEAD_DIM), DP, 0, 0, tiled=True
    ).reshape(slot_total, head_count * HEAD_DIM)
    attention = jnp.take(returned, target, axis=0)
    attention = jnp.where(my_alive[:, None] > 0, attention, jnp.zeros_like(attention))

    spread = jnp.broadcast_to(attention[None], (device_count,) + attention.shape)
    gathered = lax.all_to_all(spread, DP, 0, 0, tiled=True).reshape(
        device_count * local_beams, head_count * HEAD_DIM
    )
    partial_sum = jnp.dot(gathered, output_weight, preferred_element_type=jnp.float32)
    total_rows, out_width = partial_sum.shape
    core_count = lax.axis_size("tc")
    ring_count = lax.axis_size("tx")
    on_chip = jnp.sum(
        lax.all_to_all(
            partial_sum.reshape(core_count, total_rows // core_count, out_width), "tc", 0, 0, tiled=True
        ),
        axis=0,
    )
    chunk_rows = total_rows // (core_count * ring_count)
    reduced = jnp.sum(
        lax.all_to_all(on_chip.reshape(ring_count, chunk_rows, out_width), "tx", 0, 0, tiled=True),
        axis=0,
    ).astype(jnp.bfloat16)
    ring_copies = lax.all_to_all(
        jnp.broadcast_to(reduced[None], (ring_count,) + reduced.shape), "tx", 0, 0, tiled=True
    ).reshape(ring_count * chunk_rows, out_width)
    return lax.all_to_all(
        jnp.broadcast_to(ring_copies[None], (core_count,) + ring_copies.shape), "tc", 0, 0, tiled=True
    ).reshape(total_rows, out_width)

def solution(mesh):
    y_count = PLANE_Y
    devices = mesh.devices.reshape(y_count, mesh.devices.shape[0] // y_count, -1, 2)
    mesh = jax.sharding.Mesh(devices, ("dy", "dz", "tx", "tc"))
    placed = (
        P(DP, None),
        P(DP),
        P(DP, TP),
        P(DP, TP),
        P(DP, TP),
        P(TP, DP),
        P(DP, None, None, TP, None),
        P(),
        P(),
        P(),
    )
    return jax.shard_map(body, mesh=mesh, in_specs=placed, out_specs=P(None, DP), check_vma=False)
```

```python
import functools
import math

import jax
import jax.numpy as jnp
from jax import lax
from jax.experimental import pallas as pl
from jax.experimental.pallas import tpu as pltpu
from jax.sharding import PartitionSpec as P

HEAD_DIM = 128
SLOTS_PER_STEP = 8
PLANE_Y = 4
DP = ("dy", "dz")
TP = ("tx", "tc")


def rotate(vectors, position):
    half_width = vectors.shape[-1] // 2
    pair_index = jnp.arange(half_width).astype(jnp.float32)
    frequency = jnp.exp(pair_index * (-2.0 * math.log(1000000.0) / vectors.shape[-1]))
    angles = position.astype(jnp.float32)[:, None] * frequency[None, :]
    cosine = jnp.cos(angles)[:, None, :]
    sine_part = jnp.sin(angles)[:, None, :]
    first_half = vectors[..., :half_width]
    second = vectors[..., half_width:]
    return jnp.concatenate(
        [first_half * cosine - second * sine_part, second * cosine + first_half * sine_part],
        axis=-1,
    )


def arrival_ranks(sources):
    ordinal = jnp.arange(sources.shape[-1], dtype=jnp.int32)
    earlier = (sources[..., None, :] == sources[..., :, None]) & (
        ordinal[None, :] < ordinal[:, None]
    )
    return jnp.sum(earlier.astype(jnp.int32), axis=-1)


def attend_kernel(parent_ref, length_ref, packed_ref, *refs):
    cache_refs = refs[:-1]
    out_ref = refs[-1]
    group = len(cache_refs)
    step = pl.program_id(0)
    head_width = packed_ref.shape[-1]
    head_total = packed_ref.shape[1] - 2
    for g in range(group):
        length = length_ref[step * group + g]

        @pl.when(length == 0)
        def _():
            out_ref[g] = jnp.zeros(out_ref.shape[1:], out_ref.dtype)

        @pl.when(length > 0)
        def _():
            attend_one(packed_ref, cache_refs[g], out_ref, g, length, head_total, head_width)


def attend_one(packed_ref, cache_ref, out_ref, g, length, head_total, head_width):
    score_scale = 1.0 / math.sqrt(head_width)
    if True:
        row = packed_ref[g].astype(jnp.float32)
        queries = row[:head_total].astype(jnp.bfloat16)
        key_new = row[head_total : head_total + 1]
        value_new = row[head_total + 1 : head_total + 2]
        block = cache_ref[0]
        keys = block[:, :head_width]
        values = block[:, head_width:]
        cached = (
            lax.dot_general(
                queries, keys, (((1,), (1,)), ((), ())), preferred_element_type=jnp.float32
            )
            * score_scale
        )
        latest = (
            jnp.sum(row[:head_total] * key_new, axis=-1, keepdims=True) * score_scale
        )
        slot = lax.broadcasted_iota(jnp.int32, cached.shape, 1)
        cached = jnp.where(slot < length, cached, -jnp.inf)
        highest = jnp.maximum(jnp.max(cached, axis=-1, keepdims=True), latest)
        cached_exp = jnp.exp(cached - highest)
        latest_exp = jnp.exp(latest - highest)
        denominator = jnp.sum(cached_exp, axis=-1, keepdims=True) + latest_exp
        cached_weight = (cached_exp / denominator).astype(jnp.bfloat16)
        latest_weight = (latest_exp / denominator).astype(jnp.bfloat16)
        mixture = jnp.dot(cached_weight, values, preferred_element_type=jnp.float32)
        mixture = mixture + latest_weight.astype(jnp.float32) * value_new
        out_ref[g] = mixture.astype(out_ref.dtype)


def attend_slots(packed, cache_rows, parents, lengths):
    slot_total, rows, head_width = packed.shape
    head_total = rows - 2
    group = SLOTS_PER_STEP
    cache_len, row_width = cache_rows.shape[1], cache_rows.shape[2]

    def cache_map(g):
        return lambda i, parent_ref, length_ref: (parent_ref[i * group + g], 0, 0)

    grid_spec = pltpu.PrefetchScalarGridSpec(
        num_scalar_prefetch=2,
        grid=(slot_total // group,),
        in_specs=[pl.BlockSpec((group, rows, head_width), lambda i, p, l: (i, 0, 0))]
        + [pl.BlockSpec((1, cache_len, row_width), cache_map(g)) for g in range(group)],
        out_specs=pl.BlockSpec((group, head_total, head_width), lambda i, p, l: (i, 0, 0)),
    )
    return pl.pallas_call(
        attend_kernel,
        grid_spec=grid_spec,
        out_shape=jax.ShapeDtypeStruct((slot_total, head_total, head_width), jnp.bfloat16),
    )(parents, lengths, packed, *([cache_rows] * group))


def body(
    hidden_in,
    norm_gain,
    query_weight,
    key_weight,
    value_weight,
    output_weight,
    key_value_cache,
    cache_lengths,
    parent_beam,
    beam_alive,
):
    device_count = lax.axis_size(DP)
    device_rank = lax.axis_index(DP)
    local_beams = hidden_in.shape[0]
    capacity = max(2, (2 * local_beams + device_count - 1) // device_count)
    slot_total = device_count * capacity

    hidden_float = hidden_in.astype(jnp.float32)
    inverse = lax.rsqrt(jnp.mean(hidden_float * hidden_float, axis=1) + 1e-06)

    features = query_weight.shape[0]
    pair_count = device_count // 2
    is_low = device_rank % 2 == 0
    partner = [(i, i ^ 1) for i in range(device_count)]
    query_width = query_weight.shape[1]
    key_width = key_weight.shape[1]
    query_half = query_width // 2
    key_half = key_width // 2
    low_cols = jnp.concatenate(
        [query_weight[:, :query_half], key_weight[:, :key_half], value_weight[:, :key_half]],
        axis=1,
    )
    high_cols = jnp.concatenate(
        [query_weight[:, query_half:], key_weight[:, key_half:], value_weight[:, key_half:]],
        axis=1,
    )
    mine = jnp.where(is_low, low_cols, high_cols)
    received = lax.ppermute(jnp.where(is_low, high_cols, low_cols), DP, partner)
    partner_gain = lax.ppermute(norm_gain, DP, partner)
    pair_weight = jnp.where(
        is_low, jnp.concatenate([mine, received], 0), jnp.concatenate([received, mine], 0)
    )
    pair_gain = jnp.where(
        is_low,
        jnp.concatenate([norm_gain, partner_gain]),
        jnp.concatenate([partner_gain, norm_gain]),
    )
    spread = jnp.swapaxes(
        jnp.repeat(hidden_in.reshape(local_beams, pair_count, 2 * features), 2, axis=1), 0, 1
    )
    blocked = lax.all_to_all(spread, DP, 0, 0, tiled=True).reshape(
        device_count * local_beams, 2 * features
    )
    scaled = (blocked.astype(jnp.float32) * pair_gain.astype(jnp.float32)[None, :]).astype(
        jnp.bfloat16
    )
    partial = jnp.dot(scaled, pair_weight, preferred_element_type=jnp.float32)
    half_width = partial.shape[1]
    arrived = lax.all_to_all(
        partial.astype(jnp.bfloat16).reshape(device_count, local_beams, half_width),
        DP,
        0,
        0,
        tiled=True,
    )
    sums = jnp.sum(
        arrived.astype(jnp.float32).reshape(pair_count, 2, local_beams, half_width), axis=0
    )
    key_end = query_half + key_half
    summed = jnp.concatenate(
        [
            sums[0, :, :query_half],
            sums[1, :, :query_half],
            sums[0, :, query_half:key_end],
            sums[1, :, query_half:key_end],
            sums[0, :, key_end:],
            sums[1, :, key_end:],
        ],
        axis=1,
    ) * inverse[:, None]
    cache_rows = key_value_cache.reshape(
        local_beams, key_value_cache.shape[1], 2 * key_value_cache.shape[-1]
    )
    summed, cache_rows = lax.optimization_barrier((summed, cache_rows))

    first_beam = device_rank * local_beams
    my_parent = lax.dynamic_slice_in_dim(parent_beam, first_beam, local_beams)
    my_alive = lax.dynamic_slice_in_dim(beam_alive, first_beam, local_beams)
    position = jnp.take(cache_lengths, my_parent)
    head_count = query_width // HEAD_DIM
    group_count = key_width // HEAD_DIM
    queries = rotate(
        summed[:, :query_width].reshape(local_beams, head_count, HEAD_DIM), position
    ).astype(jnp.bfloat16)
    key_new = rotate(
        summed[:, query_width : query_width + key_width].reshape(
            local_beams, group_count, HEAD_DIM
        ),
        position,
    ).astype(jnp.bfloat16)
    value_new = (
        summed[:, query_width + key_width :]
        .reshape(local_beams, group_count, HEAD_DIM)
        .astype(jnp.bfloat16)
    )
    packed = jnp.concatenate([queries, key_new, value_new], axis=1)
    rows = packed.shape[1]

    source = my_parent // local_beams
    target = source * capacity + arrival_ranks(source)
    slot_of = jnp.arange(slot_total, dtype=jnp.int32)
    match = target[None, :] == slot_of[:, None]
    filled = jnp.any(match, axis=1)
    sender = jnp.argmax(match, axis=1)
    outgoing = jnp.where(
        filled[:, None, None], jnp.take(packed, sender, axis=0), jnp.zeros_like(packed[:1])
    )
    incoming = lax.all_to_all(
        outgoing.reshape(device_count, capacity, rows, HEAD_DIM), DP, 0, 0, tiled=True
    ).reshape(slot_total, rows, HEAD_DIM)

    all_parents = parent_beam.reshape(device_count, local_beams)
    all_sources = all_parents // local_beams
    destination = jnp.broadcast_to(
        jnp.arange(device_count, dtype=jnp.int32)[:, None], (device_count, local_beams)
    )
    placed = jnp.where(
        all_sources == device_rank, destination * capacity + arrival_ranks(all_sources), slot_total
    )
    chosen = placed.reshape(-1)[None, :] == slot_of[:, None]
    local_parent = jnp.sum(
        jnp.where(chosen, (all_parents % local_beams).reshape(-1)[None, :], 0), axis=1
    )
    used = jnp.any(chosen, axis=1).astype(jnp.int32)
    slot_length = jnp.take(cache_lengths, first_beam + local_parent) * used

    mixed = attend_slots(incoming, cache_rows, local_parent, slot_length)
    returned = lax.all_to_all(
        mixed.reshape(device_count, capacity, head_count * HEAD_DIM), DP, 0, 0, tiled=True
    ).reshape(slot_total, head_count * HEAD_DIM)
    attention = jnp.take(returned, target, axis=0)
    attention = jnp.where(my_alive[:, None] > 0, attention, jnp.zeros_like(attention))

    z_count = lax.axis_size("dz")
    y_count = lax.axis_size("dy")
    along_z = lax.all_to_all(
        jnp.broadcast_to(attention[None], (z_count,) + attention.shape), "dz", 0, 0, tiled=True
    ).reshape(z_count * local_beams, head_count * HEAD_DIM)
    gathered = lax.all_to_all(
        jnp.broadcast_to(along_z[None], (y_count,) + along_z.shape), "dy", 0, 0, tiled=True
    ).reshape(device_count * local_beams, head_count * HEAD_DIM)
    partial_sum = jnp.dot(gathered, output_weight, preferred_element_type=jnp.float32)
    total_rows, out_width = partial_sum.shape
    core_count = lax.axis_size("tc")
    ring_count = lax.axis_size("tx")
    on_chip = jnp.sum(
        lax.all_to_all(
            partial_sum.reshape(core_count, total_rows // core_count, out_width), "tc", 0, 0, tiled=True
        ),
        axis=0,
    )
    chunk_rows = total_rows // (core_count * ring_count)
    reduced = jnp.sum(
        lax.all_to_all(on_chip.reshape(ring_count, chunk_rows, out_width), "tx", 0, 0, tiled=True),
        axis=0,
    ).astype(jnp.bfloat16)
    ring_copies = lax.all_to_all(
        jnp.broadcast_to(reduced[None], (ring_count,) + reduced.shape), "tx", 0, 0, tiled=True
    ).reshape(ring_count * chunk_rows, out_width)
    return lax.all_to_all(
        jnp.broadcast_to(ring_copies[None], (core_count,) + ring_copies.shape), "tc", 0, 0, tiled=True
    ).reshape(total_rows, out_width)

def solution(mesh):
    y_count = PLANE_Y
    devices = mesh.devices.reshape(y_count, mesh.devices.shape[0] // y_count, -1, 2)
    mesh = jax.sharding.Mesh(devices, ("dy", "dz", "tx", "tc"))
    placed = (
        P(DP, None),
        P(DP),
        P(DP, TP),
        P(DP, TP),
        P(DP, TP),
        P(TP, DP),
        P(DP, None, None, TP, None),
        P(),
        P(),
        P(),
    )
    return jax.shard_map(body, mesh=mesh, in_specs=placed, out_specs=P(None, DP), check_vma=False)
```

```python
import functools
import math

import jax
import jax.numpy as jnp
from jax import lax
from jax.experimental import pallas as pl
from jax.experimental.pallas import tpu as pltpu
from jax.sharding import PartitionSpec as P

HEAD_DIM = 128
SLOTS_PER_STEP = 8
PLANE_Y = 4
DP = ("dy", "dz")
TP = ("tx", "tc")


def rotate(vectors, position):
    half_width = vectors.shape[-1] // 2
    pair_index = jnp.arange(half_width).astype(jnp.float32)
    frequency = jnp.exp(pair_index * (-2.0 * math.log(1000000.0) / vectors.shape[-1]))
    angles = position.astype(jnp.float32)[:, None] * frequency[None, :]
    cosine = jnp.cos(angles)[:, None, :]
    sine_part = jnp.sin(angles)[:, None, :]
    first_half = vectors[..., :half_width]
    second = vectors[..., half_width:]
    return jnp.concatenate(
        [first_half * cosine - second * sine_part, second * cosine + first_half * sine_part],
        axis=-1,
    )


def arrival_ranks(sources):
    ordinal = jnp.arange(sources.shape[-1], dtype=jnp.int32)
    earlier = (sources[..., None, :] == sources[..., :, None]) & (
        ordinal[None, :] < ordinal[:, None]
    )
    return jnp.sum(earlier.astype(jnp.int32), axis=-1)


def attend_kernel(parent_ref, length_ref, packed_ref, *refs):
    out_ref = refs[-1]
    group = (len(refs) - 1) // 2
    key_refs = refs[:group]
    value_refs = refs[group : 2 * group]
    step = pl.program_id(0)
    head_width = packed_ref.shape[-1]
    head_total = packed_ref.shape[1] - 2
    for g in range(group):
        length = length_ref[step * group + g]

        @pl.when(length == 0)
        def _():
            out_ref[g] = jnp.zeros(out_ref.shape[1:], out_ref.dtype)

        @pl.when(length > 0)
        def _():
            attend_one(packed_ref, key_refs[g], value_refs[g], out_ref, g, length, head_total, head_width)


def attend_one(packed_ref, key_ref, value_ref, out_ref, g, length, head_total, head_width):
    score_scale = 1.0 / math.sqrt(head_width)
    if True:
        row = packed_ref[g].astype(jnp.float32)
        queries = row[:head_total].astype(jnp.bfloat16)
        key_new = row[head_total : head_total + 1]
        value_new = row[head_total + 1 : head_total + 2]
        keys_t = key_ref[0]
        values = value_ref[0]
        cached = jnp.dot(queries, keys_t, preferred_element_type=jnp.float32) * score_scale
        latest = (
            jnp.sum(row[:head_total] * key_new, axis=-1, keepdims=True) * score_scale
        )
        slot = lax.broadcasted_iota(jnp.int32, cached.shape, 1)
        cached = jnp.where(slot < length, cached, -jnp.inf)
        highest = jnp.maximum(jnp.max(cached, axis=-1, keepdims=True), latest)
        cached_exp = jnp.exp(cached - highest)
        latest_exp = jnp.exp(latest - highest)
        denominator = jnp.sum(cached_exp, axis=-1, keepdims=True) + latest_exp
        cached_weight = (cached_exp / denominator).astype(jnp.bfloat16)
        latest_weight = (latest_exp / denominator).astype(jnp.bfloat16)
        mixture = jnp.dot(cached_weight, values, preferred_element_type=jnp.float32)
        mixture = mixture + latest_weight.astype(jnp.float32) * value_new
        out_ref[g] = mixture.astype(out_ref.dtype)


def attend_slots(packed, keys_t, values, parents, lengths):
    slot_total, rows, head_width = packed.shape
    head_total = rows - 2
    group = SLOTS_PER_STEP
    cache_len = values.shape[1]

    def cache_map(g):
        return lambda i, parent_ref, length_ref: (parent_ref[i * group + g], 0, 0)

    grid_spec = pltpu.PrefetchScalarGridSpec(
        num_scalar_prefetch=2,
        grid=(slot_total // group,),
        in_specs=[pl.BlockSpec((group, rows, head_width), lambda i, p, l: (i, 0, 0))]
        + [pl.BlockSpec((1, head_width, cache_len), cache_map(g)) for g in range(group)]
        + [pl.BlockSpec((1, cache_len, head_width), cache_map(g)) for g in range(group)],
        out_specs=pl.BlockSpec((group, head_total, head_width), lambda i, p, l: (i, 0, 0)),
    )
    return pl.pallas_call(
        attend_kernel,
        grid_spec=grid_spec,
        out_shape=jax.ShapeDtypeStruct((slot_total, head_total, head_width), jnp.bfloat16),
    )(parents, lengths, packed, *([keys_t] * group), *([values] * group))

def body(
    hidden_in,
    norm_gain,
    query_weight,
    key_weight,
    value_weight,
    output_weight,
    key_value_cache,
    cache_lengths,
    parent_beam,
    beam_alive,
):
    device_count = lax.axis_size(DP)
    device_rank = lax.axis_index(DP)
    local_beams = hidden_in.shape[0]
    capacity = max(2, (2 * local_beams + device_count - 1) // device_count)
    slot_total = device_count * capacity

    hidden_float = hidden_in.astype(jnp.float32)
    inverse = lax.rsqrt(jnp.mean(hidden_float * hidden_float, axis=1) + 1e-06)

    features = query_weight.shape[0]
    pair_count = device_count // 2
    is_low = device_rank % 2 == 0
    partner = [(i, i ^ 1) for i in range(device_count)]
    query_width = query_weight.shape[1]
    key_width = key_weight.shape[1]
    query_half = query_width // 2
    key_half = key_width // 2
    low_cols = jnp.concatenate(
        [query_weight[:, :query_half], key_weight[:, :key_half], value_weight[:, :key_half]],
        axis=1,
    )
    high_cols = jnp.concatenate(
        [query_weight[:, query_half:], key_weight[:, key_half:], value_weight[:, key_half:]],
        axis=1,
    )
    mine = jnp.where(is_low, low_cols, high_cols)
    received = lax.ppermute(jnp.where(is_low, high_cols, low_cols), DP, partner)
    partner_gain = lax.ppermute(norm_gain, DP, partner)
    pair_weight = jnp.where(
        is_low, jnp.concatenate([mine, received], 0), jnp.concatenate([received, mine], 0)
    )
    pair_gain = jnp.where(
        is_low,
        jnp.concatenate([norm_gain, partner_gain]),
        jnp.concatenate([partner_gain, norm_gain]),
    )
    spread = jnp.swapaxes(
        jnp.repeat(hidden_in.reshape(local_beams, pair_count, 2 * features), 2, axis=1), 0, 1
    )
    blocked = lax.all_to_all(spread, DP, 0, 0, tiled=True).reshape(
        device_count * local_beams, 2 * features
    )
    scaled = (blocked.astype(jnp.float32) * pair_gain.astype(jnp.float32)[None, :]).astype(
        jnp.bfloat16
    )
    partial = jnp.dot(scaled, pair_weight, preferred_element_type=jnp.float32)
    half_width = partial.shape[1]
    arrived = lax.all_to_all(
        partial.astype(jnp.bfloat16).reshape(device_count, local_beams, half_width),
        DP,
        0,
        0,
        tiled=True,
    )
    sums = jnp.sum(
        arrived.astype(jnp.float32).reshape(pair_count, 2, local_beams, half_width), axis=0
    )
    key_end = query_half + key_half
    summed = jnp.concatenate(
        [
            sums[0, :, :query_half],
            sums[1, :, :query_half],
            sums[0, :, query_half:key_end],
            sums[1, :, query_half:key_end],
            sums[0, :, key_end:],
            sums[1, :, key_end:],
        ],
        axis=1,
    ) * inverse[:, None]
    keys_t = jnp.swapaxes(key_value_cache[:, :, 0, 0, :], 1, 2)
    values = key_value_cache[:, :, 1, 0, :]
    summed, keys_t, values = lax.optimization_barrier((summed, keys_t, values))

    first_beam = device_rank * local_beams
    my_parent = lax.dynamic_slice_in_dim(parent_beam, first_beam, local_beams)
    my_alive = lax.dynamic_slice_in_dim(beam_alive, first_beam, local_beams)
    position = jnp.take(cache_lengths, my_parent)
    head_count = query_width // HEAD_DIM
    group_count = key_width // HEAD_DIM
    queries = rotate(
        summed[:, :query_width].reshape(local_beams, head_count, HEAD_DIM), position
    ).astype(jnp.bfloat16)
    key_new = rotate(
        summed[:, query_width : query_width + key_width].reshape(
            local_beams, group_count, HEAD_DIM
        ),
        position,
    ).astype(jnp.bfloat16)
    value_new = (
        summed[:, query_width + key_width :]
        .reshape(local_beams, group_count, HEAD_DIM)
        .astype(jnp.bfloat16)
    )
    packed = jnp.concatenate([queries, key_new, value_new], axis=1)
    rows = packed.shape[1]

    source = my_parent // local_beams
    target = source * capacity + arrival_ranks(source)
    slot_of = jnp.arange(slot_total, dtype=jnp.int32)
    match = target[None, :] == slot_of[:, None]
    filled = jnp.any(match, axis=1)
    sender = jnp.argmax(match, axis=1)
    outgoing = jnp.where(
        filled[:, None, None], jnp.take(packed, sender, axis=0), jnp.zeros_like(packed[:1])
    )
    incoming = lax.all_to_all(
        outgoing.reshape(device_count, capacity, rows, HEAD_DIM), DP, 0, 0, tiled=True
    ).reshape(slot_total, rows, HEAD_DIM)

    all_parents = parent_beam.reshape(device_count, local_beams)
    all_sources = all_parents // local_beams
    destination = jnp.broadcast_to(
        jnp.arange(device_count, dtype=jnp.int32)[:, None], (device_count, local_beams)
    )
    placed = jnp.where(
        all_sources == device_rank, destination * capacity + arrival_ranks(all_sources), slot_total
    )
    chosen = placed.reshape(-1)[None, :] == slot_of[:, None]
    local_parent = jnp.sum(
        jnp.where(chosen, (all_parents % local_beams).reshape(-1)[None, :], 0), axis=1
    )
    used = jnp.any(chosen, axis=1).astype(jnp.int32)
    slot_length = jnp.take(cache_lengths, first_beam + local_parent) * used

    mixed = attend_slots(incoming, keys_t, values, local_parent, slot_length)
    returned = lax.all_to_all(
        mixed.reshape(device_count, capacity, head_count * HEAD_DIM), DP, 0, 0, tiled=True
    ).reshape(slot_total, head_count * HEAD_DIM)
    attention = jnp.take(returned, target, axis=0)
    attention = jnp.where(my_alive[:, None] > 0, attention, jnp.zeros_like(attention))

    z_count = lax.axis_size("dz")
    y_count = lax.axis_size("dy")
    along_z = lax.all_to_all(
        jnp.broadcast_to(attention[None], (z_count,) + attention.shape), "dz", 0, 0, tiled=True
    ).reshape(z_count * local_beams, head_count * HEAD_DIM)
    gathered = lax.all_to_all(
        jnp.broadcast_to(along_z[None], (y_count,) + along_z.shape), "dy", 0, 0, tiled=True
    ).reshape(device_count * local_beams, head_count * HEAD_DIM)
    partial_sum = jnp.dot(gathered, output_weight, preferred_element_type=jnp.float32)
    total_rows, out_width = partial_sum.shape
    core_count = lax.axis_size("tc")
    ring_count = lax.axis_size("tx")
    on_chip = jnp.sum(
        lax.all_to_all(
            partial_sum.reshape(core_count, total_rows // core_count, out_width), "tc", 0, 0, tiled=True
        ),
        axis=0,
    )
    chunk_rows = total_rows // (core_count * ring_count)
    reduced = jnp.sum(
        lax.all_to_all(on_chip.reshape(ring_count, chunk_rows, out_width), "tx", 0, 0, tiled=True),
        axis=0,
    ).astype(jnp.bfloat16)
    ring_copies = lax.all_to_all(
        jnp.broadcast_to(reduced[None], (ring_count,) + reduced.shape), "tx", 0, 0, tiled=True
    ).reshape(ring_count * chunk_rows, out_width)
    return lax.all_to_all(
        jnp.broadcast_to(ring_copies[None], (core_count,) + ring_copies.shape), "tc", 0, 0, tiled=True
    ).reshape(total_rows, out_width)

def solution(mesh):
    y_count = PLANE_Y
    devices = mesh.devices.reshape(y_count, mesh.devices.shape[0] // y_count, -1, 2)
    mesh = jax.sharding.Mesh(devices, ("dy", "dz", "tx", "tc"))
    placed = (
        P(DP, None),
        P(DP),
        P(DP, TP),
        P(DP, TP),
        P(DP, TP),
        P(TP, DP),
        P(DP, None, None, TP, None),
        P(),
        P(),
        P(),
    )
    return jax.shard_map(body, mesh=mesh, in_specs=placed, out_specs=P(None, DP), check_vma=False)
```

```python
import functools
import math

import jax
import jax.numpy as jnp
from jax import lax
from jax.experimental import pallas as pl
from jax.experimental.pallas import tpu as pltpu
from jax.sharding import PartitionSpec as P

HEAD_DIM = 128
SLOTS_PER_STEP = 8
PLANE_Y = 4
DP = ("dy", "dz")
TP = ("tx", "tc")


def rotate(vectors, position):
    half_width = vectors.shape[-1] // 2
    pair_index = jnp.arange(half_width).astype(jnp.float32)
    frequency = jnp.exp(pair_index * (-2.0 * math.log(1000000.0) / vectors.shape[-1]))
    angles = position.astype(jnp.float32)[:, None] * frequency[None, :]
    cosine = jnp.cos(angles)[:, None, :]
    sine_part = jnp.sin(angles)[:, None, :]
    first_half = vectors[..., :half_width]
    second = vectors[..., half_width:]
    return jnp.concatenate(
        [first_half * cosine - second * sine_part, second * cosine + first_half * sine_part],
        axis=-1,
    )


def arrival_ranks(sources):
    ordinal = jnp.arange(sources.shape[-1], dtype=jnp.int32)
    earlier = (sources[..., None, :] == sources[..., :, None]) & (
        ordinal[None, :] < ordinal[:, None]
    )
    return jnp.sum(earlier.astype(jnp.int32), axis=-1)


def attend_kernel(parent_ref, length_ref, packed_ref, *refs):
    out_ref = refs[-1]
    group = (len(refs) - 1) // 2
    key_refs = refs[:group]
    value_refs = refs[group : 2 * group]
    step = pl.program_id(0)
    head_width = packed_ref.shape[-1]
    head_total = packed_ref.shape[1] - 2
    @pl.when(length_ref[step * group] == 0)
    def _():
        out_ref[...] = jnp.zeros(out_ref.shape, out_ref.dtype)

    @pl.when(length_ref[step * group] > 0)
    def _():
        for g in range(group):
            length = length_ref[step * group + g]
            attend_one(packed_ref, key_refs[g], value_refs[g], out_ref, g, length, head_total, head_width)


def attend_one(packed_ref, key_ref, value_ref, out_ref, g, length, head_total, head_width):
    score_scale = 1.0 / math.sqrt(head_width)
    if True:
        row = packed_ref[g].astype(jnp.float32)
        queries = row[:head_total].astype(jnp.bfloat16)
        key_new = row[head_total : head_total + 1]
        value_new = row[head_total + 1 : head_total + 2]
        keys_t = key_ref[0]
        values = value_ref[0]
        cached = jnp.dot(queries, keys_t, preferred_element_type=jnp.float32) * score_scale
        latest = (
            jnp.sum(row[:head_total] * key_new, axis=-1, keepdims=True) * score_scale
        )
        slot = lax.broadcasted_iota(jnp.int32, cached.shape, 1)
        cached = jnp.where(slot < length, cached, -jnp.inf)
        highest = jnp.maximum(jnp.max(cached, axis=-1, keepdims=True), latest)
        cached_exp = jnp.exp(cached - highest)
        latest_exp = jnp.exp(latest - highest)
        denominator = jnp.sum(cached_exp, axis=-1, keepdims=True) + latest_exp
        cached_weight = (cached_exp / denominator).astype(jnp.bfloat16)
        latest_weight = (latest_exp / denominator).astype(jnp.bfloat16)
        mixture = jnp.dot(cached_weight, values, preferred_element_type=jnp.float32)
        mixture = mixture + latest_weight.astype(jnp.float32) * value_new
        out_ref[g] = mixture.astype(out_ref.dtype)


def attend_slots(packed, keys_t, values, parents, lengths):
    slot_total, rows, head_width = packed.shape
    head_total = rows - 2
    group = SLOTS_PER_STEP
    cache_len = values.shape[1]

    def cache_map(g):
        return lambda i, parent_ref, length_ref: (parent_ref[i * group + g], 0, 0)

    grid_spec = pltpu.PrefetchScalarGridSpec(
        num_scalar_prefetch=2,
        grid=(slot_total // group,),
        in_specs=[pl.BlockSpec((group, rows, head_width), lambda i, p, l: (i, 0, 0))]
        + [pl.BlockSpec((1, head_width, cache_len), cache_map(g)) for g in range(group)]
        + [pl.BlockSpec((1, cache_len, head_width), cache_map(g)) for g in range(group)],
        out_specs=pl.BlockSpec((group, head_total, head_width), lambda i, p, l: (i, 0, 0)),
    )
    return pl.pallas_call(
        attend_kernel,
        grid_spec=grid_spec,
        out_shape=jax.ShapeDtypeStruct((slot_total, head_total, head_width), jnp.bfloat16),
    )(parents, lengths, packed, *([keys_t] * group), *([values] * group))

def body(
    hidden_in,
    norm_gain,
    query_weight,
    key_weight,
    value_weight,
    output_weight,
    key_value_cache,
    cache_lengths,
    parent_beam,
    beam_alive,
):
    device_count = lax.axis_size(DP)
    device_rank = lax.axis_index(DP)
    local_beams = hidden_in.shape[0]
    capacity = max(2, (2 * local_beams + device_count - 1) // device_count)
    slot_total = device_count * capacity

    hidden_float = hidden_in.astype(jnp.float32)
    inverse = lax.rsqrt(jnp.mean(hidden_float * hidden_float, axis=1) + 1e-06)

    features = query_weight.shape[0]
    pair_count = device_count // 2
    is_low = device_rank % 2 == 0
    partner = [(i, i ^ 1) for i in range(device_count)]
    query_width = query_weight.shape[1]
    key_width = key_weight.shape[1]
    query_half = query_width // 2
    key_half = key_width // 2
    low_cols = jnp.concatenate(
        [query_weight[:, :query_half], key_weight[:, :key_half], value_weight[:, :key_half]],
        axis=1,
    )
    high_cols = jnp.concatenate(
        [query_weight[:, query_half:], key_weight[:, key_half:], value_weight[:, key_half:]],
        axis=1,
    )
    mine = jnp.where(is_low, low_cols, high_cols)
    received = lax.ppermute(jnp.where(is_low, high_cols, low_cols), DP, partner)
    partner_gain = lax.ppermute(norm_gain, DP, partner)
    pair_weight = jnp.where(
        is_low, jnp.concatenate([mine, received], 0), jnp.concatenate([received, mine], 0)
    )
    pair_gain = jnp.where(
        is_low,
        jnp.concatenate([norm_gain, partner_gain]),
        jnp.concatenate([partner_gain, norm_gain]),
    )
    spread = jnp.swapaxes(
        jnp.repeat(hidden_in.reshape(local_beams, pair_count, 2 * features), 2, axis=1), 0, 1
    )
    blocked = lax.all_to_all(spread, DP, 0, 0, tiled=True).reshape(
        device_count * local_beams, 2 * features
    )
    scaled = (blocked.astype(jnp.float32) * pair_gain.astype(jnp.float32)[None, :]).astype(
        jnp.bfloat16
    )
    partial = jnp.dot(scaled, pair_weight, preferred_element_type=jnp.float32)
    half_width = partial.shape[1]
    arrived = lax.all_to_all(
        partial.astype(jnp.bfloat16).reshape(device_count, local_beams, half_width),
        DP,
        0,
        0,
        tiled=True,
    )
    sums = jnp.sum(
        arrived.astype(jnp.float32).reshape(pair_count, 2, local_beams, half_width), axis=0
    )
    key_end = query_half + key_half
    summed = jnp.concatenate(
        [
            sums[0, :, :query_half],
            sums[1, :, :query_half],
            sums[0, :, query_half:key_end],
            sums[1, :, query_half:key_end],
            sums[0, :, key_end:],
            sums[1, :, key_end:],
        ],
        axis=1,
    ) * inverse[:, None]
    keys_t = jnp.swapaxes(key_value_cache[:, :, 0, 0, :], 1, 2)
    values = key_value_cache[:, :, 1, 0, :]
    summed, keys_t, values = lax.optimization_barrier((summed, keys_t, values))

    first_beam = device_rank * local_beams
    my_parent = lax.dynamic_slice_in_dim(parent_beam, first_beam, local_beams)
    my_alive = lax.dynamic_slice_in_dim(beam_alive, first_beam, local_beams)
    position = jnp.take(cache_lengths, my_parent)
    head_count = query_width // HEAD_DIM
    group_count = key_width // HEAD_DIM
    queries = rotate(
        summed[:, :query_width].reshape(local_beams, head_count, HEAD_DIM), position
    ).astype(jnp.bfloat16)
    key_new = rotate(
        summed[:, query_width : query_width + key_width].reshape(
            local_beams, group_count, HEAD_DIM
        ),
        position,
    ).astype(jnp.bfloat16)
    value_new = (
        summed[:, query_width + key_width :]
        .reshape(local_beams, group_count, HEAD_DIM)
        .astype(jnp.bfloat16)
    )
    packed = jnp.concatenate([queries, key_new, value_new], axis=1)
    rows = packed.shape[1]

    source = my_parent // local_beams
    target = source * capacity + arrival_ranks(source)
    slot_of = jnp.arange(slot_total, dtype=jnp.int32)
    match = target[None, :] == slot_of[:, None]
    filled = jnp.any(match, axis=1)
    sender = jnp.argmax(match, axis=1)
    outgoing = jnp.where(
        filled[:, None, None], jnp.take(packed, sender, axis=0), jnp.zeros_like(packed[:1])
    )
    incoming = lax.all_to_all(
        outgoing.reshape(device_count, capacity, rows, HEAD_DIM), DP, 0, 0, tiled=True
    ).reshape(slot_total, rows, HEAD_DIM)

    all_parents = parent_beam.reshape(device_count, local_beams)
    all_sources = all_parents // local_beams
    destination = jnp.broadcast_to(
        jnp.arange(device_count, dtype=jnp.int32)[:, None], (device_count, local_beams)
    )
    placed = jnp.where(
        all_sources == device_rank, destination * capacity + arrival_ranks(all_sources), slot_total
    )
    chosen = placed.reshape(-1)[None, :] == slot_of[:, None]
    local_parent = jnp.sum(
        jnp.where(chosen, (all_parents % local_beams).reshape(-1)[None, :], 0), axis=1
    )
    used = jnp.any(chosen, axis=1).astype(jnp.int32)
    slot_length = jnp.take(cache_lengths, first_beam + local_parent) * used

    real_rank = jnp.cumsum(used) - 1
    pad_rank = jnp.sum(used) + jnp.cumsum(1 - used) - 1
    order = jnp.where(used > 0, real_rank, pad_rank)
    moved = order[None, :] == slot_of[:, None]
    sorted_from = jnp.sum(jnp.where(moved, slot_of[None, :], 0), axis=1)
    mixed_sorted = attend_slots(
        jnp.take(incoming, sorted_from, axis=0),
        keys_t,
        values,
        jnp.take(local_parent, sorted_from),
        jnp.take(slot_length, sorted_from),
    )
    mixed = jnp.take(mixed_sorted, order, axis=0)
    returned = lax.all_to_all(
        mixed.reshape(device_count, capacity, head_count * HEAD_DIM), DP, 0, 0, tiled=True
    ).reshape(slot_total, head_count * HEAD_DIM)
    attention = jnp.take(returned, target, axis=0)
    attention = jnp.where(my_alive[:, None] > 0, attention, jnp.zeros_like(attention))

    z_count = lax.axis_size("dz")
    y_count = lax.axis_size("dy")
    along_z = lax.all_to_all(
        jnp.broadcast_to(attention[None], (z_count,) + attention.shape), "dz", 0, 0, tiled=True
    ).reshape(z_count * local_beams, head_count * HEAD_DIM)
    gathered = lax.all_to_all(
        jnp.broadcast_to(along_z[None], (y_count,) + along_z.shape), "dy", 0, 0, tiled=True
    ).reshape(device_count * local_beams, head_count * HEAD_DIM)
    partial_sum = jnp.dot(gathered, output_weight, preferred_element_type=jnp.float32)
    total_rows, out_width = partial_sum.shape
    core_count = lax.axis_size("tc")
    ring_count = lax.axis_size("tx")
    on_chip = jnp.sum(
        lax.all_to_all(
            partial_sum.reshape(core_count, total_rows // core_count, out_width), "tc", 0, 0, tiled=True
        ),
        axis=0,
    )
    chunk_rows = total_rows // (core_count * ring_count)
    reduced = jnp.sum(
        lax.all_to_all(on_chip.reshape(ring_count, chunk_rows, out_width), "tx", 0, 0, tiled=True),
        axis=0,
    ).astype(jnp.bfloat16)
    ring_copies = lax.all_to_all(
        jnp.broadcast_to(reduced[None], (ring_count,) + reduced.shape), "tx", 0, 0, tiled=True
    ).reshape(ring_count * chunk_rows, out_width)
    return lax.all_to_all(
        jnp.broadcast_to(ring_copies[None], (core_count,) + ring_copies.shape), "tc", 0, 0, tiled=True
    ).reshape(total_rows, out_width)

def solution(mesh):
    y_count = PLANE_Y
    devices = mesh.devices.reshape(y_count, mesh.devices.shape[0] // y_count, -1, 2)
    mesh = jax.sharding.Mesh(devices, ("dy", "dz", "tx", "tc"))
    placed = (
        P(DP, None),
        P(DP),
        P(DP, TP),
        P(DP, TP),
        P(DP, TP),
        P(TP, DP),
        P(DP, None, None, TP, None),
        P(),
        P(),
        P(),
    )
    return jax.shard_map(body, mesh=mesh, in_specs=placed, out_specs=P(None, DP), check_vma=False)
```

```python
import functools
import math

import jax
import jax.numpy as jnp
from jax import lax
from jax.experimental import pallas as pl
from jax.experimental.pallas import tpu as pltpu
from jax.sharding import PartitionSpec as P

HEAD_DIM = 128
SLOTS_PER_STEP = 8
PLANE_Y = 4
DP = ("dy", "dz")
TP = ("tx", "tc")


def rotate(vectors, position):
    half_width = vectors.shape[-1] // 2
    pair_index = jnp.arange(half_width).astype(jnp.float32)
    frequency = jnp.exp(pair_index * (-2.0 * math.log(1000000.0) / vectors.shape[-1]))
    angles = position.astype(jnp.float32)[:, None] * frequency[None, :]
    cosine = jnp.cos(angles)[:, None, :]
    sine_part = jnp.sin(angles)[:, None, :]
    first_half = vectors[..., :half_width]
    second = vectors[..., half_width:]
    return jnp.concatenate(
        [first_half * cosine - second * sine_part, second * cosine + first_half * sine_part],
        axis=-1,
    )


def arrival_ranks(sources):
    ordinal = jnp.arange(sources.shape[-1], dtype=jnp.int32)
    earlier = (sources[..., None, :] == sources[..., :, None]) & (
        ordinal[None, :] < ordinal[:, None]
    )
    return jnp.sum(earlier.astype(jnp.int32), axis=-1)


def attend_kernel(parent_ref, length_ref, packed_ref, *refs):
    out_ref = refs[-1]
    group = (len(refs) - 1) // 2
    key_refs = refs[:group]
    value_refs = refs[group : 2 * group]
    step = pl.program_id(0)
    head_width = packed_ref.shape[-1]
    head_total = packed_ref.shape[1] - 2
    @pl.when(length_ref[step * group] == 0)
    def _():
        out_ref[...] = jnp.zeros(out_ref.shape, out_ref.dtype)

    @pl.when(length_ref[step * group] > 0)
    def _():
        for g in range(group):
            length = length_ref[step * group + g]
            attend_one(packed_ref, key_refs[g], value_refs[g], out_ref, g, length, head_total, head_width)


def attend_one(packed_ref, key_ref, value_ref, out_ref, g, length, head_total, head_width):
    score_scale = 1.0 / math.sqrt(head_width)
    if True:
        row = packed_ref[g].astype(jnp.float32)
        queries = row[:head_total].astype(jnp.bfloat16)
        key_new = row[head_total : head_total + 1]
        value_new = row[head_total + 1 : head_total + 2]
        keys_t = key_ref[0]
        values = value_ref[0]
        cached = jnp.dot(queries, keys_t, preferred_element_type=jnp.float32) * score_scale
        latest = (
            jnp.sum(row[:head_total] * key_new, axis=-1, keepdims=True) * score_scale
        )
        slot = lax.broadcasted_iota(jnp.int32, cached.shape, 1)
        cached = jnp.where(slot < length, cached, -jnp.inf)
        highest = jnp.maximum(jnp.max(cached, axis=-1, keepdims=True), latest)
        cached_exp = jnp.exp(cached - highest)
        latest_exp = jnp.exp(latest - highest)
        denominator = jnp.sum(cached_exp, axis=-1, keepdims=True) + latest_exp
        cached_weight = (cached_exp / denominator).astype(jnp.bfloat16)
        latest_weight = (latest_exp / denominator).astype(jnp.bfloat16)
        mixture = jnp.dot(cached_weight, values, preferred_element_type=jnp.float32)
        mixture = mixture + latest_weight.astype(jnp.float32) * value_new
        out_ref[g] = mixture.astype(out_ref.dtype)


def attend_slots(packed, keys_t, values, parents, lengths):
    slot_total, rows, head_width = packed.shape
    head_total = rows - 2
    group = SLOTS_PER_STEP
    cache_len = values.shape[1]

    def cache_map(g):
        return lambda i, parent_ref, length_ref: (parent_ref[i * group + g], 0, 0)

    grid_spec = pltpu.PrefetchScalarGridSpec(
        num_scalar_prefetch=2,
        grid=(slot_total // group,),
        in_specs=[pl.BlockSpec((group, rows, head_width), lambda i, p, l: (i, 0, 0))]
        + [pl.BlockSpec((1, head_width, cache_len), cache_map(g)) for g in range(group)]
        + [pl.BlockSpec((1, cache_len, head_width), cache_map(g)) for g in range(group)],
        out_specs=pl.BlockSpec((group, head_total, head_width), lambda i, p, l: (i, 0, 0)),
    )
    return pl.pallas_call(
        attend_kernel,
        grid_spec=grid_spec,
        out_shape=jax.ShapeDtypeStruct((slot_total, head_total, head_width), jnp.bfloat16),
    )(parents, lengths, packed, *([keys_t] * group), *([values] * group))

def body(
    hidden_in,
    norm_gain,
    query_weight,
    key_weight,
    value_weight,
    output_weight,
    key_value_cache,
    cache_lengths,
    parent_beam,
    beam_alive,
):
    device_count = lax.axis_size(DP)
    device_rank = lax.axis_index(DP)
    local_beams = hidden_in.shape[0]
    capacity = max(2, (2 * local_beams + device_count - 1) // device_count)
    slot_total = device_count * capacity

    hidden_float = hidden_in.astype(jnp.float32)
    inverse = lax.rsqrt(jnp.mean(hidden_float * hidden_float, axis=1) + 1e-06)

    features = query_weight.shape[0]
    pair_count = device_count // 2
    is_low = device_rank % 2 == 0
    partner = [(i, i ^ 1) for i in range(device_count)]
    query_width = query_weight.shape[1]
    key_width = key_weight.shape[1]
    query_half = query_width // 2
    key_half = key_width // 2
    low_cols = jnp.concatenate(
        [query_weight[:, :query_half], key_weight[:, :key_half], value_weight[:, :key_half]],
        axis=1,
    )
    high_cols = jnp.concatenate(
        [query_weight[:, query_half:], key_weight[:, key_half:], value_weight[:, key_half:]],
        axis=1,
    )
    mine = jnp.where(is_low, low_cols, high_cols)
    received = lax.ppermute(jnp.where(is_low, high_cols, low_cols), DP, partner)
    partner_gain = lax.ppermute(norm_gain, DP, partner)
    pair_weight = jnp.where(
        is_low, jnp.concatenate([mine, received], 0), jnp.concatenate([received, mine], 0)
    )
    pair_gain = jnp.where(
        is_low,
        jnp.concatenate([norm_gain, partner_gain]),
        jnp.concatenate([partner_gain, norm_gain]),
    )
    spread = jnp.swapaxes(
        jnp.repeat(hidden_in.reshape(local_beams, pair_count, 2 * features), 2, axis=1), 0, 1
    )
    blocked = lax.all_to_all(spread, DP, 0, 0, tiled=True).reshape(
        device_count * local_beams, 2 * features
    )
    scaled = (blocked.astype(jnp.float32) * pair_gain.astype(jnp.float32)[None, :]).astype(
        jnp.bfloat16
    )
    partial = jnp.dot(scaled, pair_weight, preferred_element_type=jnp.float32)
    half_width = partial.shape[1]
    arrived = lax.all_to_all(
        partial.astype(jnp.bfloat16).reshape(device_count, local_beams, half_width),
        DP,
        0,
        0,
        tiled=True,
    )
    sums = jnp.sum(
        arrived.astype(jnp.float32).reshape(pair_count, 2, local_beams, half_width), axis=0
    )
    key_end = query_half + key_half
    summed = jnp.concatenate(
        [
            sums[0, :, :query_half],
            sums[1, :, :query_half],
            sums[0, :, query_half:key_end],
            sums[1, :, query_half:key_end],
            sums[0, :, key_end:],
            sums[1, :, key_end:],
        ],
        axis=1,
    ) * inverse[:, None]
    keys_t = jnp.swapaxes(key_value_cache[:, :, 0, 0, :], 1, 2)
    values = key_value_cache[:, :, 1, 0, :]
    summed, keys_t, values = lax.optimization_barrier((summed, keys_t, values))

    first_beam = device_rank * local_beams
    my_parent = lax.dynamic_slice_in_dim(parent_beam, first_beam, local_beams)
    my_alive = lax.dynamic_slice_in_dim(beam_alive, first_beam, local_beams)
    position = jnp.take(cache_lengths, my_parent)
    head_count = query_width // HEAD_DIM
    group_count = key_width // HEAD_DIM
    queries = rotate(
        summed[:, :query_width].reshape(local_beams, head_count, HEAD_DIM), position
    ).astype(jnp.bfloat16)
    key_new = rotate(
        summed[:, query_width : query_width + key_width].reshape(
            local_beams, group_count, HEAD_DIM
        ),
        position,
    ).astype(jnp.bfloat16)
    value_new = (
        summed[:, query_width + key_width :]
        .reshape(local_beams, group_count, HEAD_DIM)
        .astype(jnp.bfloat16)
    )
    packed = jnp.concatenate([queries, key_new, value_new], axis=1)
    rows = packed.shape[1]

    source = my_parent // local_beams
    target = source * capacity + arrival_ranks(source)
    slot_of = jnp.arange(slot_total, dtype=jnp.int32)
    match = target[None, :] == slot_of[:, None]
    filled = jnp.any(match, axis=1)
    sender = jnp.argmax(match, axis=1)
    outgoing = jnp.where(
        filled[:, None, None], jnp.take(packed, sender, axis=0), jnp.zeros_like(packed[:1])
    )
    incoming = lax.all_to_all(
        outgoing.reshape(device_count, capacity, rows, HEAD_DIM), DP, 0, 0, tiled=True
    ).reshape(slot_total, rows, HEAD_DIM)

    all_parents = parent_beam.reshape(device_count, local_beams)
    all_sources = all_parents // local_beams
    destination = jnp.broadcast_to(
        jnp.arange(device_count, dtype=jnp.int32)[:, None], (device_count, local_beams)
    )
    placed = jnp.where(
        all_sources == device_rank, destination * capacity + arrival_ranks(all_sources), slot_total
    )
    chosen = placed.reshape(-1)[None, :] == slot_of[:, None]
    local_parent = jnp.sum(
        jnp.where(chosen, (all_parents % local_beams).reshape(-1)[None, :], 0), axis=1
    )
    used = jnp.any(chosen, axis=1).astype(jnp.int32)
    slot_length = jnp.take(cache_lengths, first_beam + local_parent) * used

    real_rank = jnp.cumsum(used) - 1
    pad_rank = jnp.sum(used) + jnp.cumsum(1 - used) - 1
    order = jnp.where(used > 0, real_rank, pad_rank)
    moved = order[None, :] == slot_of[:, None]
    sorted_from = jnp.sum(jnp.where(moved, slot_of[None, :], 0), axis=1)
    mixed_sorted = attend_slots(
        jnp.take(incoming, sorted_from, axis=0),
        keys_t,
        values,
        jnp.take(local_parent, sorted_from),
        jnp.take(slot_length, sorted_from),
    )
    mixed = jnp.take(mixed_sorted, order, axis=0)
    returned = lax.all_to_all(
        mixed.reshape(device_count, capacity, head_count * HEAD_DIM), DP, 0, 0, tiled=True
    ).reshape(slot_total, head_count * HEAD_DIM)
    attention = jnp.take(returned, target, axis=0)
    attention = jnp.where(my_alive[:, None] > 0, attention, jnp.zeros_like(attention))

    tensor_count = lax.axis_size(TP)
    tensor_rank = lax.axis_index(TP)
    share = local_beams // tensor_count
    width = head_count * HEAD_DIM
    heads_all = lax.all_to_all(
        attention.reshape(tensor_count, share, width), TP, 0, 0, tiled=True
    )
    mine = jnp.swapaxes(heads_all, 0, 1).reshape(share, tensor_count * width)
    z_count = lax.axis_size("dz")
    y_count = lax.axis_size("dy")
    along_z = lax.all_to_all(
        jnp.broadcast_to(mine[None], (z_count,) + mine.shape), "dz", 0, 0, tiled=True
    ).reshape(z_count * share, tensor_count * width)
    gathered = lax.all_to_all(
        jnp.broadcast_to(along_z[None], (y_count,) + along_z.shape), "dy", 0, 0, tiled=True
    ).reshape(device_count * share, tensor_count * width)
    blocks = output_weight
    bit = 1
    while bit < tensor_count:
        pairs = [(i, i ^ bit) for i in range(tensor_count)]
        blocks = jnp.concatenate([blocks, lax.ppermute(blocks, TP, pairs)], axis=0)
        bit *= 2
    rows_per = output_weight.shape[0]
    order = jnp.arange(tensor_count, dtype=jnp.int32) ^ tensor_rank
    full_weight = jnp.take(
        blocks.reshape(tensor_count, rows_per, output_weight.shape[1]), order, axis=0
    ).reshape(tensor_count * rows_per, output_weight.shape[1])
    out_rows = jnp.dot(gathered, full_weight, preferred_element_type=jnp.float32).astype(
        jnp.bfloat16
    )
    out_width = out_rows.shape[1]
    copies = lax.all_to_all(
        jnp.broadcast_to(out_rows[None], (tensor_count,) + out_rows.shape), TP, 0, 0, tiled=True
    )
    return jnp.swapaxes(
        copies.reshape(tensor_count, device_count, share, out_width), 0, 1
    ).reshape(device_count * local_beams, out_width)

def solution(mesh):
    y_count = PLANE_Y
    devices = mesh.devices.reshape(y_count, mesh.devices.shape[0] // y_count, -1, 2)
    mesh = jax.sharding.Mesh(devices, ("dy", "dz", "tx", "tc"))
    placed = (
        P(DP, None),
        P(DP),
        P(DP, TP),
        P(DP, TP),
        P(DP, TP),
        P(TP, DP),
        P(DP, None, None, TP, None),
        P(),
        P(),
        P(),
    )
    return jax.shard_map(body, mesh=mesh, in_specs=placed, out_specs=P(None, DP), check_vma=False)
```

```python
import functools
import math

import jax
import jax.numpy as jnp
from jax import lax
from jax.experimental import pallas as pl
from jax.experimental.pallas import tpu as pltpu
from jax.sharding import PartitionSpec as P

HEAD_DIM = 128
SLOTS_PER_STEP = 8
PLANE_Y = 4
DP = ("dy", "dz")
TP = ("tx", "tc")


def rotate(vectors, position):
    half_width = vectors.shape[-1] // 2
    pair_index = jnp.arange(half_width).astype(jnp.float32)
    frequency = jnp.exp(pair_index * (-2.0 * math.log(1000000.0) / vectors.shape[-1]))
    angles = position.astype(jnp.float32)[:, None] * frequency[None, :]
    cosine = jnp.cos(angles)[:, None, :]
    sine_part = jnp.sin(angles)[:, None, :]
    first_half = vectors[..., :half_width]
    second = vectors[..., half_width:]
    return jnp.concatenate(
        [first_half * cosine - second * sine_part, second * cosine + first_half * sine_part],
        axis=-1,
    )


def arrival_ranks(sources):
    ordinal = jnp.arange(sources.shape[-1], dtype=jnp.int32)
    earlier = (sources[..., None, :] == sources[..., :, None]) & (
        ordinal[None, :] < ordinal[:, None]
    )
    return jnp.sum(earlier.astype(jnp.int32), axis=-1)


def attend_kernel(parent_ref, length_ref, packed_ref, *refs):
    out_ref = refs[-1]
    group = (len(refs) - 1) // 2
    key_refs = refs[:group]
    value_refs = refs[group : 2 * group]
    step = pl.program_id(0)
    head_width = packed_ref.shape[-1]
    head_total = packed_ref.shape[1] - 2
    @pl.when(length_ref[step * group] == 0)
    def _():
        out_ref[...] = jnp.zeros(out_ref.shape, out_ref.dtype)

    @pl.when(length_ref[step * group] > 0)
    def _():
        for g in range(group):
            length = length_ref[step * group + g]
            attend_one(packed_ref, key_refs[g], value_refs[g], out_ref, g, length, head_total, head_width)


def attend_one(packed_ref, key_ref, value_ref, out_ref, g, length, head_total, head_width):
    score_scale = 1.0 / math.sqrt(head_width)
    if True:
        row = packed_ref[g].astype(jnp.float32)
        queries = row[:head_total].astype(jnp.bfloat16)
        key_new = row[head_total : head_total + 1]
        value_new = row[head_total + 1 : head_total + 2]
        keys_t = key_ref[0]
        values = value_ref[0]
        cached = jnp.dot(queries, keys_t, preferred_element_type=jnp.float32) * score_scale
        latest = (
            jnp.sum(row[:head_total] * key_new, axis=-1, keepdims=True) * score_scale
        )
        slot = lax.broadcasted_iota(jnp.int32, cached.shape, 1)
        cached = jnp.where(slot < length, cached, -jnp.inf)
        highest = jnp.maximum(jnp.max(cached, axis=-1, keepdims=True), latest)
        cached_exp = jnp.exp(cached - highest)
        latest_exp = jnp.exp(latest - highest)
        denominator = jnp.sum(cached_exp, axis=-1, keepdims=True) + latest_exp
        cached_weight = (cached_exp / denominator).astype(jnp.bfloat16)
        latest_weight = (latest_exp / denominator).astype(jnp.bfloat16)
        mixture = jnp.dot(cached_weight, values, preferred_element_type=jnp.float32)
        mixture = mixture + latest_weight.astype(jnp.float32) * value_new
        out_ref[g] = mixture.astype(out_ref.dtype)


def attend_slots(packed, keys_t, values, parents, lengths):
    slot_total, rows, head_width = packed.shape
    head_total = rows - 2
    group = SLOTS_PER_STEP
    cache_len = values.shape[1]

    def cache_map(g):
        return lambda i, parent_ref, length_ref: (parent_ref[i * group + g], 0, 0)

    grid_spec = pltpu.PrefetchScalarGridSpec(
        num_scalar_prefetch=2,
        grid=(slot_total // group,),
        in_specs=[pl.BlockSpec((group, rows, head_width), lambda i, p, l: (i, 0, 0))]
        + [pl.BlockSpec((1, head_width, cache_len), cache_map(g)) for g in range(group)]
        + [pl.BlockSpec((1, cache_len, head_width), cache_map(g)) for g in range(group)],
        out_specs=pl.BlockSpec((group, head_total, head_width), lambda i, p, l: (i, 0, 0)),
    )
    return pl.pallas_call(
        attend_kernel,
        grid_spec=grid_spec,
        out_shape=jax.ShapeDtypeStruct((slot_total, head_total, head_width), jnp.bfloat16),
    )(parents, lengths, packed, *([keys_t] * group), *([values] * group))

def body(
    hidden_in,
    norm_gain,
    query_weight,
    key_weight,
    value_weight,
    output_weight,
    key_value_cache,
    cache_lengths,
    parent_beam,
    beam_alive,
):
    device_count = lax.axis_size(DP)
    device_rank = lax.axis_index(DP)
    local_beams = hidden_in.shape[0]
    capacity = max(2, (2 * local_beams + device_count - 1) // device_count)
    slot_total = device_count * capacity

    hidden_float = hidden_in.astype(jnp.float32)
    inverse = lax.rsqrt(jnp.mean(hidden_float * hidden_float, axis=1) + 1e-06)

    features = query_weight.shape[0]
    pair_count = device_count // 2
    is_low = device_rank % 2 == 0
    partner = [(i, i ^ 1) for i in range(device_count)]
    query_width = query_weight.shape[1]
    key_width = key_weight.shape[1]
    query_half = query_width // 2
    key_half = key_width // 2
    low_cols = jnp.concatenate(
        [query_weight[:, :query_half], key_weight[:, :key_half], value_weight[:, :key_half]],
        axis=1,
    )
    high_cols = jnp.concatenate(
        [query_weight[:, query_half:], key_weight[:, key_half:], value_weight[:, key_half:]],
        axis=1,
    )
    mine = jnp.where(is_low, low_cols, high_cols)
    received = lax.ppermute(jnp.where(is_low, high_cols, low_cols), DP, partner)
    partner_gain = lax.ppermute(norm_gain, DP, partner)
    pair_weight = jnp.where(
        is_low, jnp.concatenate([mine, received], 0), jnp.concatenate([received, mine], 0)
    )
    pair_gain = jnp.where(
        is_low,
        jnp.concatenate([norm_gain, partner_gain]),
        jnp.concatenate([partner_gain, norm_gain]),
    )
    spread = jnp.swapaxes(hidden_in.reshape(local_beams, device_count, features), 0, 1)
    own_rows = lax.all_to_all(spread, DP, 0, 0, tiled=True).reshape(
        device_count * local_beams, features
    )
    partner_rows = lax.ppermute(own_rows, DP, partner)
    blocked = jnp.where(
        is_low,
        jnp.concatenate([own_rows, partner_rows], 1),
        jnp.concatenate([partner_rows, own_rows], 1),
    )
    scaled = (blocked.astype(jnp.float32) * pair_gain.astype(jnp.float32)[None, :]).astype(
        jnp.bfloat16
    )
    partial = jnp.dot(scaled, pair_weight, preferred_element_type=jnp.float32)
    half_width = partial.shape[1]
    arrived = lax.all_to_all(
        partial.astype(jnp.bfloat16).reshape(device_count, local_beams, half_width),
        DP,
        0,
        0,
        tiled=True,
    )
    sums = jnp.sum(
        arrived.astype(jnp.float32).reshape(pair_count, 2, local_beams, half_width), axis=0
    )
    key_end = query_half + key_half
    summed = jnp.concatenate(
        [
            sums[0, :, :query_half],
            sums[1, :, :query_half],
            sums[0, :, query_half:key_end],
            sums[1, :, query_half:key_end],
            sums[0, :, key_end:],
            sums[1, :, key_end:],
        ],
        axis=1,
    ) * inverse[:, None]
    keys_t = jnp.swapaxes(key_value_cache[:, :, 0, 0, :], 1, 2)
    values = key_value_cache[:, :, 1, 0, :]
    summed, keys_t, values = lax.optimization_barrier((summed, keys_t, values))

    first_beam = device_rank * local_beams
    my_parent = lax.dynamic_slice_in_dim(parent_beam, first_beam, local_beams)
    my_alive = lax.dynamic_slice_in_dim(beam_alive, first_beam, local_beams)
    position = jnp.take(cache_lengths, my_parent)
    head_count = query_width // HEAD_DIM
    group_count = key_width // HEAD_DIM
    queries = rotate(
        summed[:, :query_width].reshape(local_beams, head_count, HEAD_DIM), position
    ).astype(jnp.bfloat16)
    key_new = rotate(
        summed[:, query_width : query_width + key_width].reshape(
            local_beams, group_count, HEAD_DIM
        ),
        position,
    ).astype(jnp.bfloat16)
    value_new = (
        summed[:, query_width + key_width :]
        .reshape(local_beams, group_count, HEAD_DIM)
        .astype(jnp.bfloat16)
    )
    packed = jnp.concatenate([queries, key_new, value_new], axis=1)
    rows = packed.shape[1]

    source = my_parent // local_beams
    target = source * capacity + arrival_ranks(source)
    slot_of = jnp.arange(slot_total, dtype=jnp.int32)
    match = target[None, :] == slot_of[:, None]
    filled = jnp.any(match, axis=1)
    sender = jnp.argmax(match, axis=1)
    outgoing = jnp.where(
        filled[:, None, None], jnp.take(packed, sender, axis=0), jnp.zeros_like(packed[:1])
    )
    incoming = lax.all_to_all(
        outgoing.reshape(device_count, capacity, rows, HEAD_DIM), DP, 0, 0, tiled=True
    ).reshape(slot_total, rows, HEAD_DIM)

    all_parents = parent_beam.reshape(device_count, local_beams)
    all_sources = all_parents // local_beams
    destination = jnp.broadcast_to(
        jnp.arange(device_count, dtype=jnp.int32)[:, None], (device_count, local_beams)
    )
    placed = jnp.where(
        all_sources == device_rank, destination * capacity + arrival_ranks(all_sources), slot_total
    )
    chosen = placed.reshape(-1)[None, :] == slot_of[:, None]
    local_parent = jnp.sum(
        jnp.where(chosen, (all_parents % local_beams).reshape(-1)[None, :], 0), axis=1
    )
    used = jnp.any(chosen, axis=1).astype(jnp.int32)
    slot_length = jnp.take(cache_lengths, first_beam + local_parent) * used

    real_rank = jnp.cumsum(used) - 1
    pad_rank = jnp.sum(used) + jnp.cumsum(1 - used) - 1
    order = jnp.where(used > 0, real_rank, pad_rank)
    moved = order[None, :] == slot_of[:, None]
    sorted_from = jnp.sum(jnp.where(moved, slot_of[None, :], 0), axis=1)
    mixed_sorted = attend_slots(
        jnp.take(incoming, sorted_from, axis=0),
        keys_t,
        values,
        jnp.take(local_parent, sorted_from),
        jnp.take(slot_length, sorted_from),
    )
    mixed = jnp.take(mixed_sorted, order, axis=0)
    returned = lax.all_to_all(
        mixed.reshape(device_count, capacity, head_count * HEAD_DIM), DP, 0, 0, tiled=True
    ).reshape(slot_total, head_count * HEAD_DIM)
    attention = jnp.take(returned, target, axis=0)
    attention = jnp.where(my_alive[:, None] > 0, attention, jnp.zeros_like(attention))

    z_count = lax.axis_size("dz")
    y_count = lax.axis_size("dy")
    along_z = lax.all_to_all(
        jnp.broadcast_to(attention[None], (z_count,) + attention.shape), "dz", 0, 0, tiled=True
    ).reshape(z_count * local_beams, head_count * HEAD_DIM)
    gathered = lax.all_to_all(
        jnp.broadcast_to(along_z[None], (y_count,) + along_z.shape), "dy", 0, 0, tiled=True
    ).reshape(device_count * local_beams, head_count * HEAD_DIM)
    partial_sum = jnp.dot(gathered, output_weight, preferred_element_type=jnp.float32)
    total_rows, out_width = partial_sum.shape
    core_count = lax.axis_size("tc")
    ring_count = lax.axis_size("tx")
    on_chip = jnp.sum(
        lax.all_to_all(
            partial_sum.reshape(core_count, total_rows // core_count, out_width), "tc", 0, 0, tiled=True
        ),
        axis=0,
    )
    chunk_rows = total_rows // (core_count * ring_count)
    reduced = jnp.sum(
        lax.all_to_all(on_chip.reshape(ring_count, chunk_rows, out_width), "tx", 0, 0, tiled=True),
        axis=0,
    ).astype(jnp.bfloat16)
    ring_copies = lax.all_to_all(
        jnp.broadcast_to(reduced[None], (ring_count,) + reduced.shape), "tx", 0, 0, tiled=True
    ).reshape(ring_count * chunk_rows, out_width)
    return lax.all_to_all(
        jnp.broadcast_to(ring_copies[None], (core_count,) + ring_copies.shape), "tc", 0, 0, tiled=True
    ).reshape(total_rows, out_width)

def solution(mesh):
    y_count = PLANE_Y
    devices = mesh.devices.reshape(y_count, mesh.devices.shape[0] // y_count, -1, 2)
    mesh = jax.sharding.Mesh(devices, ("dy", "dz", "tx", "tc"))
    placed = (
        P(DP, None),
        P(DP),
        P(DP, TP),
        P(DP, TP),
        P(DP, TP),
        P(TP, DP),
        P(DP, None, None, TP, None),
        P(),
        P(),
        P(),
    )
    return jax.shard_map(body, mesh=mesh, in_specs=placed, out_specs=P(None, DP), check_vma=False)
```

```python
import functools
import math

import jax
import jax.numpy as jnp
from jax import lax
from jax.experimental import pallas as pl
from jax.experimental.pallas import tpu as pltpu
from jax.sharding import PartitionSpec as P

HEAD_DIM = 128
SLOTS_PER_STEP = 8
PLANE_Y = 4
DP = ("dy", "dz")
TP = ("tx", "tc")


def rotate(vectors, position):
    half_width = vectors.shape[-1] // 2
    pair_index = jnp.arange(half_width).astype(jnp.float32)
    frequency = jnp.exp(pair_index * (-2.0 * math.log(1000000.0) / vectors.shape[-1]))
    angles = position.astype(jnp.float32)[:, None] * frequency[None, :]
    cosine = jnp.cos(angles)[:, None, :]
    sine_part = jnp.sin(angles)[:, None, :]
    first_half = vectors[..., :half_width]
    second = vectors[..., half_width:]
    return jnp.concatenate(
        [first_half * cosine - second * sine_part, second * cosine + first_half * sine_part],
        axis=-1,
    )


def arrival_ranks(sources):
    ordinal = jnp.arange(sources.shape[-1], dtype=jnp.int32)
    earlier = (sources[..., None, :] == sources[..., :, None]) & (
        ordinal[None, :] < ordinal[:, None]
    )
    return jnp.sum(earlier.astype(jnp.int32), axis=-1)


def attend_kernel(parent_ref, length_ref, packed_ref, *refs):
    out_ref = refs[-1]
    group = (len(refs) - 1) // 2
    key_refs = refs[:group]
    value_refs = refs[group : 2 * group]
    step = pl.program_id(0)
    head_width = packed_ref.shape[-1]
    head_total = packed_ref.shape[1] - 2
    @pl.when(length_ref[step * group] == 0)
    def _():
        out_ref[...] = jnp.zeros(out_ref.shape, out_ref.dtype)

    @pl.when(length_ref[step * group] > 0)
    def _():
        for g in range(group):
            length = length_ref[step * group + g]
            attend_one(packed_ref, key_refs[g], value_refs[g], out_ref, g, length, head_total, head_width)


def attend_one(packed_ref, key_ref, value_ref, out_ref, g, length, head_total, head_width):
    score_scale = 1.0 / math.sqrt(head_width)
    if True:
        row = packed_ref[g].astype(jnp.float32)
        queries = row[:head_total].astype(jnp.bfloat16)
        key_new = row[head_total : head_total + 1]
        value_new = row[head_total + 1 : head_total + 2]
        keys_t = key_ref[0]
        values = value_ref[0]
        cached = jnp.dot(queries, keys_t, preferred_element_type=jnp.float32) * score_scale
        latest = (
            jnp.sum(row[:head_total] * key_new, axis=-1, keepdims=True) * score_scale
        )
        slot = lax.broadcasted_iota(jnp.int32, cached.shape, 1)
        cached = jnp.where(slot < length, cached, -jnp.inf)
        highest = jnp.maximum(jnp.max(cached, axis=-1, keepdims=True), latest)
        cached_exp = jnp.exp(cached - highest)
        latest_exp = jnp.exp(latest - highest)
        denominator = jnp.sum(cached_exp, axis=-1, keepdims=True) + latest_exp
        cached_weight = (cached_exp / denominator).astype(jnp.bfloat16)
        latest_weight = (latest_exp / denominator).astype(jnp.bfloat16)
        mixture = jnp.dot(cached_weight, values, preferred_element_type=jnp.float32)
        mixture = mixture + latest_weight.astype(jnp.float32) * value_new
        out_ref[g] = mixture.astype(out_ref.dtype)


def attend_slots(packed, keys_t, values, parents, lengths):
    slot_total, rows, head_width = packed.shape
    head_total = rows - 2
    group = SLOTS_PER_STEP
    cache_len = values.shape[1]

    def cache_map(g):
        return lambda i, parent_ref, length_ref: (parent_ref[i * group + g], 0, 0)

    grid_spec = pltpu.PrefetchScalarGridSpec(
        num_scalar_prefetch=2,
        grid=(slot_total // group,),
        in_specs=[pl.BlockSpec((group, rows, head_width), lambda i, p, l: (i, 0, 0))]
        + [pl.BlockSpec((1, head_width, cache_len), cache_map(g)) for g in range(group)]
        + [pl.BlockSpec((1, cache_len, head_width), cache_map(g)) for g in range(group)],
        out_specs=pl.BlockSpec((group, head_total, head_width), lambda i, p, l: (i, 0, 0)),
    )
    return pl.pallas_call(
        attend_kernel,
        grid_spec=grid_spec,
        out_shape=jax.ShapeDtypeStruct((slot_total, head_total, head_width), jnp.bfloat16),
    )(parents, lengths, packed, *([keys_t] * group), *([values] * group))

def body(
    hidden_in,
    norm_gain,
    query_weight,
    key_weight,
    value_weight,
    output_weight,
    key_value_cache,
    cache_lengths,
    parent_beam,
    beam_alive,
):
    device_count = lax.axis_size(DP)
    device_rank = lax.axis_index(DP)
    local_beams = hidden_in.shape[0]
    capacity = max(2, (2 * local_beams + device_count - 1) // device_count)
    slot_total = device_count * capacity

    hidden_float = hidden_in.astype(jnp.float32)
    inverse = lax.rsqrt(jnp.mean(hidden_float * hidden_float, axis=1) + 1e-06)

    features = query_weight.shape[0]
    z_count = device_count // PLANE_Y
    is_low = (device_rank // z_count) % 2 == 0
    partner = [(i, i ^ z_count) for i in range(device_count)]
    query_width = query_weight.shape[1]
    key_width = key_weight.shape[1]
    query_half = query_width // 2
    key_half = key_width // 2
    low_cols = jnp.concatenate(
        [query_weight[:, :query_half], key_weight[:, :key_half], value_weight[:, :key_half]],
        axis=1,
    )
    high_cols = jnp.concatenate(
        [query_weight[:, query_half:], key_weight[:, key_half:], value_weight[:, key_half:]],
        axis=1,
    )
    mine = jnp.where(is_low, low_cols, high_cols)
    received = lax.ppermute(jnp.where(is_low, high_cols, low_cols), DP, partner)
    partner_gain = lax.ppermute(norm_gain, DP, partner)
    pair_weight = jnp.where(
        is_low, jnp.concatenate([mine, received], 0), jnp.concatenate([received, mine], 0)
    )
    pair_gain = jnp.where(
        is_low,
        jnp.concatenate([norm_gain, partner_gain]),
        jnp.concatenate([partner_gain, norm_gain]),
    )
    pair_blocks = jnp.swapaxes(
        hidden_in.reshape(local_beams, PLANE_Y // 2, 2, z_count, features), 2, 3
    ).reshape(local_beams, PLANE_Y // 2, 1, z_count, 2 * features)
    spread = jnp.swapaxes(
        jnp.broadcast_to(
            pair_blocks, (local_beams, PLANE_Y // 2, 2, z_count, 2 * features)
        ).reshape(local_beams, device_count, 2 * features),
        0,
        1,
    )
    blocked = lax.all_to_all(spread, DP, 0, 0, tiled=True).reshape(
        device_count * local_beams, 2 * features
    )
    scaled = (blocked.astype(jnp.float32) * pair_gain.astype(jnp.float32)[None, :]).astype(
        jnp.bfloat16
    )
    partial = jnp.dot(scaled, pair_weight, preferred_element_type=jnp.float32)
    half_width = partial.shape[1]
    arrived = lax.all_to_all(
        partial.astype(jnp.bfloat16).reshape(device_count, local_beams, half_width),
        DP,
        0,
        0,
        tiled=True,
    )
    sums = jnp.sum(
        arrived.astype(jnp.float32).reshape(
            PLANE_Y // 2, 2, z_count, local_beams, half_width
        ),
        axis=(0, 2),
    )
    key_end = query_half + key_half
    summed = jnp.concatenate(
        [
            sums[0, :, :query_half],
            sums[1, :, :query_half],
            sums[0, :, query_half:key_end],
            sums[1, :, query_half:key_end],
            sums[0, :, key_end:],
            sums[1, :, key_end:],
        ],
        axis=1,
    ) * inverse[:, None]
    keys_t = jnp.swapaxes(key_value_cache[:, :, 0, 0, :], 1, 2)
    values = key_value_cache[:, :, 1, 0, :]
    summed, keys_t, values = lax.optimization_barrier((summed, keys_t, values))

    first_beam = device_rank * local_beams
    my_parent = lax.dynamic_slice_in_dim(parent_beam, first_beam, local_beams)
    my_alive = lax.dynamic_slice_in_dim(beam_alive, first_beam, local_beams)
    position = jnp.take(cache_lengths, my_parent)
    head_count = query_width // HEAD_DIM
    group_count = key_width // HEAD_DIM
    queries = rotate(
        summed[:, :query_width].reshape(local_beams, head_count, HEAD_DIM), position
    ).astype(jnp.bfloat16)
    key_new = rotate(
        summed[:, query_width : query_width + key_width].reshape(
            local_beams, group_count, HEAD_DIM
        ),
        position,
    ).astype(jnp.bfloat16)
    value_new = (
        summed[:, query_width + key_width :]
        .reshape(local_beams, group_count, HEAD_DIM)
        .astype(jnp.bfloat16)
    )
    packed = jnp.concatenate([queries, key_new, value_new], axis=1)
    rows = packed.shape[1]

    source = my_parent // local_beams
    target = source * capacity + arrival_ranks(source)
    slot_of = jnp.arange(slot_total, dtype=jnp.int32)
    match = target[None, :] == slot_of[:, None]
    filled = jnp.any(match, axis=1)
    sender = jnp.argmax(match, axis=1)
    outgoing = jnp.where(
        filled[:, None, None], jnp.take(packed, sender, axis=0), jnp.zeros_like(packed[:1])
    )
    incoming = lax.all_to_all(
        outgoing.reshape(device_count, capacity, rows, HEAD_DIM), DP, 0, 0, tiled=True
    ).reshape(slot_total, rows, HEAD_DIM)

    all_parents = parent_beam.reshape(device_count, local_beams)
    all_sources = all_parents // local_beams
    destination = jnp.broadcast_to(
        jnp.arange(device_count, dtype=jnp.int32)[:, None], (device_count, local_beams)
    )
    placed = jnp.where(
        all_sources == device_rank, destination * capacity + arrival_ranks(all_sources), slot_total
    )
    chosen = placed.reshape(-1)[None, :] == slot_of[:, None]
    local_parent = jnp.sum(
        jnp.where(chosen, (all_parents % local_beams).reshape(-1)[None, :], 0), axis=1
    )
    used = jnp.any(chosen, axis=1).astype(jnp.int32)
    slot_length = jnp.take(cache_lengths, first_beam + local_parent) * used

    real_rank = jnp.cumsum(used) - 1
    pad_rank = jnp.sum(used) + jnp.cumsum(1 - used) - 1
    order = jnp.where(used > 0, real_rank, pad_rank)
    moved = order[None, :] == slot_of[:, None]
    sorted_from = jnp.sum(jnp.where(moved, slot_of[None, :], 0), axis=1)
    mixed_sorted = attend_slots(
        jnp.take(incoming, sorted_from, axis=0),
        keys_t,
        values,
        jnp.take(local_parent, sorted_from),
        jnp.take(slot_length, sorted_from),
    )
    mixed = jnp.take(mixed_sorted, order, axis=0)
    returned = lax.all_to_all(
        mixed.reshape(device_count, capacity, head_count * HEAD_DIM), DP, 0, 0, tiled=True
    ).reshape(slot_total, head_count * HEAD_DIM)
    attention = jnp.take(returned, target, axis=0)
    attention = jnp.where(my_alive[:, None] > 0, attention, jnp.zeros_like(attention))

    z_count = lax.axis_size("dz")
    y_count = lax.axis_size("dy")
    along_z = lax.all_to_all(
        jnp.broadcast_to(attention[None], (z_count,) + attention.shape), "dz", 0, 0, tiled=True
    ).reshape(z_count * local_beams, head_count * HEAD_DIM)
    gathered = lax.all_to_all(
        jnp.broadcast_to(along_z[None], (y_count,) + along_z.shape), "dy", 0, 0, tiled=True
    ).reshape(device_count * local_beams, head_count * HEAD_DIM)
    partial_sum = jnp.dot(gathered, output_weight, preferred_element_type=jnp.float32)
    total_rows, out_width = partial_sum.shape
    core_count = lax.axis_size("tc")
    ring_count = lax.axis_size("tx")
    on_chip = jnp.sum(
        lax.all_to_all(
            partial_sum.reshape(core_count, total_rows // core_count, out_width), "tc", 0, 0, tiled=True
        ),
        axis=0,
    )
    chunk_rows = total_rows // (core_count * ring_count)
    reduced = jnp.sum(
        lax.all_to_all(on_chip.reshape(ring_count, chunk_rows, out_width), "tx", 0, 0, tiled=True),
        axis=0,
    ).astype(jnp.bfloat16)
    ring_copies = lax.all_to_all(
        jnp.broadcast_to(reduced[None], (ring_count,) + reduced.shape), "tx", 0, 0, tiled=True
    ).reshape(ring_count * chunk_rows, out_width)
    return lax.all_to_all(
        jnp.broadcast_to(ring_copies[None], (core_count,) + ring_copies.shape), "tc", 0, 0, tiled=True
    ).reshape(total_rows, out_width)

def solution(mesh):
    y_count = PLANE_Y
    devices = mesh.devices.reshape(y_count, mesh.devices.shape[0] // y_count, -1, 2)
    mesh = jax.sharding.Mesh(devices, ("dy", "dz", "tx", "tc"))
    placed = (
        P(DP, None),
        P(DP),
        P(DP, TP),
        P(DP, TP),
        P(DP, TP),
        P(TP, DP),
        P(DP, None, None, TP, None),
        P(),
        P(),
        P(),
    )
    return jax.shard_map(body, mesh=mesh, in_specs=placed, out_specs=P(None, DP), check_vma=False)
```

```python
import functools
import math

import jax
import jax.numpy as jnp
from jax import lax
from jax.experimental import pallas as pl
from jax.experimental.pallas import tpu as pltpu
from jax.sharding import PartitionSpec as P

HEAD_DIM = 128
SLOTS_PER_STEP = 16
PLANE_Y = 4
DP = ("dy", "dz")
TP = ("tx", "tc")


def rotate(vectors, position):
    half_width = vectors.shape[-1] // 2
    pair_index = jnp.arange(half_width).astype(jnp.float32)
    frequency = jnp.exp(pair_index * (-2.0 * math.log(1000000.0) / vectors.shape[-1]))
    angles = position.astype(jnp.float32)[:, None] * frequency[None, :]
    cosine = jnp.cos(angles)[:, None, :]
    sine_part = jnp.sin(angles)[:, None, :]
    first_half = vectors[..., :half_width]
    second = vectors[..., half_width:]
    return jnp.concatenate(
        [first_half * cosine - second * sine_part, second * cosine + first_half * sine_part],
        axis=-1,
    )


def arrival_ranks(sources):
    ordinal = jnp.arange(sources.shape[-1], dtype=jnp.int32)
    earlier = (sources[..., None, :] == sources[..., :, None]) & (
        ordinal[None, :] < ordinal[:, None]
    )
    return jnp.sum(earlier.astype(jnp.int32), axis=-1)


def attend_kernel(parent_ref, length_ref, packed_ref, *refs):
    out_ref = refs[-1]
    group = (len(refs) - 1) // 2
    key_refs = refs[:group]
    value_refs = refs[group : 2 * group]
    step = pl.program_id(0)
    head_width = packed_ref.shape[-1]
    head_total = packed_ref.shape[1] - 2
    @pl.when(length_ref[step * group] == 0)
    def _():
        out_ref[...] = jnp.zeros(out_ref.shape, out_ref.dtype)

    @pl.when(length_ref[step * group] > 0)
    def _():
        for g in range(group):
            length = length_ref[step * group + g]
            attend_one(packed_ref, key_refs[g], value_refs[g], out_ref, g, length, head_total, head_width)


def attend_one(packed_ref, key_ref, value_ref, out_ref, g, length, head_total, head_width):
    score_scale = 1.0 / math.sqrt(head_width)
    if True:
        row = packed_ref[g].astype(jnp.float32)
        queries = row[:head_total].astype(jnp.bfloat16)
        key_new = row[head_total : head_total + 1]
        value_new = row[head_total + 1 : head_total + 2]
        keys_t = key_ref[0]
        values = value_ref[0]
        cached = jnp.dot(queries, keys_t, preferred_element_type=jnp.float32) * score_scale
        latest = (
            jnp.sum(row[:head_total] * key_new, axis=-1, keepdims=True) * score_scale
        )
        slot = lax.broadcasted_iota(jnp.int32, cached.shape, 1)
        cached = jnp.where(slot < length, cached, -jnp.inf)
        highest = jnp.maximum(jnp.max(cached, axis=-1, keepdims=True), latest)
        cached_exp = jnp.exp(cached - highest)
        latest_exp = jnp.exp(latest - highest)
        denominator = jnp.sum(cached_exp, axis=-1, keepdims=True) + latest_exp
        cached_weight = (cached_exp / denominator).astype(jnp.bfloat16)
        latest_weight = (latest_exp / denominator).astype(jnp.bfloat16)
        mixture = jnp.dot(cached_weight, values, preferred_element_type=jnp.float32)
        mixture = mixture + latest_weight.astype(jnp.float32) * value_new
        out_ref[g] = mixture.astype(out_ref.dtype)


def attend_slots(packed, keys_t, values, parents, lengths):
    slot_total, rows, head_width = packed.shape
    head_total = rows - 2
    group = SLOTS_PER_STEP
    cache_len = values.shape[1]

    def cache_map(g):
        return lambda i, parent_ref, length_ref: (parent_ref[i * group + g], 0, 0)

    grid_spec = pltpu.PrefetchScalarGridSpec(
        num_scalar_prefetch=2,
        grid=(slot_total // group,),
        in_specs=[pl.BlockSpec((group, rows, head_width), lambda i, p, l: (i, 0, 0))]
        + [pl.BlockSpec((1, head_width, cache_len), cache_map(g)) for g in range(group)]
        + [pl.BlockSpec((1, cache_len, head_width), cache_map(g)) for g in range(group)],
        out_specs=pl.BlockSpec((group, head_total, head_width), lambda i, p, l: (i, 0, 0)),
    )
    return pl.pallas_call(
        attend_kernel,
        grid_spec=grid_spec,
        out_shape=jax.ShapeDtypeStruct((slot_total, head_total, head_width), jnp.bfloat16),
    )(parents, lengths, packed, *([keys_t] * group), *([values] * group))

def body(
    hidden_in,
    norm_gain,
    query_weight,
    key_weight,
    value_weight,
    output_weight,
    key_value_cache,
    cache_lengths,
    parent_beam,
    beam_alive,
):
    device_count = lax.axis_size(DP)
    device_rank = lax.axis_index(DP)
    local_beams = hidden_in.shape[0]
    capacity = max(2, (2 * local_beams + device_count - 1) // device_count)
    slot_total = device_count * capacity

    hidden_float = hidden_in.astype(jnp.float32)
    inverse = lax.rsqrt(jnp.mean(hidden_float * hidden_float, axis=1) + 1e-06)

    features = query_weight.shape[0]
    pair_count = device_count // 2
    is_low = device_rank % 2 == 0
    partner = [(i, i ^ 1) for i in range(device_count)]
    query_width = query_weight.shape[1]
    key_width = key_weight.shape[1]
    query_half = query_width // 2
    key_half = key_width // 2
    low_cols = jnp.concatenate(
        [query_weight[:, :query_half], key_weight[:, :key_half], value_weight[:, :key_half]],
        axis=1,
    )
    high_cols = jnp.concatenate(
        [query_weight[:, query_half:], key_weight[:, key_half:], value_weight[:, key_half:]],
        axis=1,
    )
    mine = jnp.where(is_low, low_cols, high_cols)
    received = lax.ppermute(jnp.where(is_low, high_cols, low_cols), DP, partner)
    partner_gain = lax.ppermute(norm_gain, DP, partner)
    pair_weight = jnp.where(
        is_low, jnp.concatenate([mine, received], 0), jnp.concatenate([received, mine], 0)
    )
    pair_gain = jnp.where(
        is_low,
        jnp.concatenate([norm_gain, partner_gain]),
        jnp.concatenate([partner_gain, norm_gain]),
    )
    spread = jnp.swapaxes(
        jnp.repeat(hidden_in.reshape(local_beams, pair_count, 2 * features), 2, axis=1), 0, 1
    )
    blocked = lax.all_to_all(spread, DP, 0, 0, tiled=True).reshape(
        device_count * local_beams, 2 * features
    )
    scaled = (blocked.astype(jnp.float32) * pair_gain.astype(jnp.float32)[None, :]).astype(
        jnp.bfloat16
    )
    partial = jnp.dot(scaled, pair_weight, preferred_element_type=jnp.float32)
    half_width = partial.shape[1]
    arrived = lax.all_to_all(
        partial.astype(jnp.bfloat16).reshape(device_count, local_beams, half_width),
        DP,
        0,
        0,
        tiled=True,
    )
    sums = jnp.sum(
        arrived.astype(jnp.float32).reshape(pair_count, 2, local_beams, half_width), axis=0
    )
    key_end = query_half + key_half
    summed = jnp.concatenate(
        [
            sums[0, :, :query_half],
            sums[1, :, :query_half],
            sums[0, :, query_half:key_end],
            sums[1, :, query_half:key_end],
            sums[0, :, key_end:],
            sums[1, :, key_end:],
        ],
        axis=1,
    ) * inverse[:, None]
    keys_t = jnp.swapaxes(key_value_cache[:, :, 0, 0, :], 1, 2)
    values = key_value_cache[:, :, 1, 0, :]
    summed, keys_t, values = lax.optimization_barrier((summed, keys_t, values))

    first_beam = device_rank * local_beams
    my_parent = lax.dynamic_slice_in_dim(parent_beam, first_beam, local_beams)
    my_alive = lax.dynamic_slice_in_dim(beam_alive, first_beam, local_beams)
    position = jnp.take(cache_lengths, my_parent)
    head_count = query_width // HEAD_DIM
    group_count = key_width // HEAD_DIM
    queries = rotate(
        summed[:, :query_width].reshape(local_beams, head_count, HEAD_DIM), position
    ).astype(jnp.bfloat16)
    key_new = rotate(
        summed[:, query_width : query_width + key_width].reshape(
            local_beams, group_count, HEAD_DIM
        ),
        position,
    ).astype(jnp.bfloat16)
    value_new = (
        summed[:, query_width + key_width :]
        .reshape(local_beams, group_count, HEAD_DIM)
        .astype(jnp.bfloat16)
    )
    packed = jnp.concatenate([queries, key_new, value_new], axis=1)
    rows = packed.shape[1]

    source = my_parent // local_beams
    target = source * capacity + arrival_ranks(source)
    slot_of = jnp.arange(slot_total, dtype=jnp.int32)
    match = target[None, :] == slot_of[:, None]
    filled = jnp.any(match, axis=1)
    sender = jnp.argmax(match, axis=1)
    outgoing = jnp.where(
        filled[:, None, None], jnp.take(packed, sender, axis=0), jnp.zeros_like(packed[:1])
    )
    incoming = lax.all_to_all(
        outgoing.reshape(device_count, capacity, rows, HEAD_DIM), DP, 0, 0, tiled=True
    ).reshape(slot_total, rows, HEAD_DIM)

    all_parents = parent_beam.reshape(device_count, local_beams)
    all_sources = all_parents // local_beams
    destination = jnp.broadcast_to(
        jnp.arange(device_count, dtype=jnp.int32)[:, None], (device_count, local_beams)
    )
    placed = jnp.where(
        all_sources == device_rank, destination * capacity + arrival_ranks(all_sources), slot_total
    )
    chosen = placed.reshape(-1)[None, :] == slot_of[:, None]
    local_parent = jnp.sum(
        jnp.where(chosen, (all_parents % local_beams).reshape(-1)[None, :], 0), axis=1
    )
    used = jnp.any(chosen, axis=1).astype(jnp.int32)
    slot_length = jnp.take(cache_lengths, first_beam + local_parent) * used

    real_rank = jnp.cumsum(used) - 1
    pad_rank = jnp.sum(used) + jnp.cumsum(1 - used) - 1
    order = jnp.where(used > 0, real_rank, pad_rank)
    moved = order[None, :] == slot_of[:, None]
    sorted_from = jnp.sum(jnp.where(moved, slot_of[None, :], 0), axis=1)
    mixed_sorted = attend_slots(
        jnp.take(incoming, sorted_from, axis=0),
        keys_t,
        values,
        jnp.take(local_parent, sorted_from),
        jnp.take(slot_length, sorted_from),
    )
    mixed = jnp.take(mixed_sorted, order, axis=0)
    returned = lax.all_to_all(
        mixed.reshape(device_count, capacity, head_count * HEAD_DIM), DP, 0, 0, tiled=True
    ).reshape(slot_total, head_count * HEAD_DIM)
    attention = jnp.take(returned, target, axis=0)
    attention = jnp.where(my_alive[:, None] > 0, attention, jnp.zeros_like(attention))

    z_count = lax.axis_size("dz")
    y_count = lax.axis_size("dy")
    along_z = lax.all_to_all(
        jnp.broadcast_to(attention[None], (z_count,) + attention.shape), "dz", 0, 0, tiled=True
    ).reshape(z_count * local_beams, head_count * HEAD_DIM)
    gathered = lax.all_to_all(
        jnp.broadcast_to(along_z[None], (y_count,) + along_z.shape), "dy", 0, 0, tiled=True
    ).reshape(device_count * local_beams, head_count * HEAD_DIM)
    partial_sum = jnp.dot(gathered, output_weight, preferred_element_type=jnp.float32)
    total_rows, out_width = partial_sum.shape
    core_count = lax.axis_size("tc")
    ring_count = lax.axis_size("tx")
    on_chip = jnp.sum(
        lax.all_to_all(
            partial_sum.reshape(core_count, total_rows // core_count, out_width), "tc", 0, 0, tiled=True
        ),
        axis=0,
    )
    chunk_rows = total_rows // (core_count * ring_count)
    reduced = jnp.sum(
        lax.all_to_all(on_chip.reshape(ring_count, chunk_rows, out_width), "tx", 0, 0, tiled=True),
        axis=0,
    ).astype(jnp.bfloat16)
    ring_copies = lax.all_to_all(
        jnp.broadcast_to(reduced[None], (ring_count,) + reduced.shape), "tx", 0, 0, tiled=True
    ).reshape(ring_count * chunk_rows, out_width)
    return lax.all_to_all(
        jnp.broadcast_to(ring_copies[None], (core_count,) + ring_copies.shape), "tc", 0, 0, tiled=True
    ).reshape(total_rows, out_width)

def solution(mesh):
    y_count = PLANE_Y
    devices = mesh.devices.reshape(y_count, mesh.devices.shape[0] // y_count, -1, 2)
    mesh = jax.sharding.Mesh(devices, ("dy", "dz", "tx", "tc"))
    placed = (
        P(DP, None),
        P(DP),
        P(DP, TP),
        P(DP, TP),
        P(DP, TP),
        P(TP, DP),
        P(DP, None, None, TP, None),
        P(),
        P(),
        P(),
    )
    return jax.shard_map(body, mesh=mesh, in_specs=placed, out_specs=P(None, DP), check_vma=False)
```

```python
import functools
import math

import jax
import jax.numpy as jnp
from jax import lax
from jax.experimental import pallas as pl
from jax.experimental.pallas import tpu as pltpu
from jax.sharding import PartitionSpec as P

HEAD_DIM = 128
SLOTS_PER_STEP = 32
PLANE_Y = 4
DP = ("dy", "dz")
TP = ("tx", "tc")


def rotate(vectors, position):
    half_width = vectors.shape[-1] // 2
    pair_index = jnp.arange(half_width).astype(jnp.float32)
    frequency = jnp.exp(pair_index * (-2.0 * math.log(1000000.0) / vectors.shape[-1]))
    angles = position.astype(jnp.float32)[:, None] * frequency[None, :]
    cosine = jnp.cos(angles)[:, None, :]
    sine_part = jnp.sin(angles)[:, None, :]
    first_half = vectors[..., :half_width]
    second = vectors[..., half_width:]
    return jnp.concatenate(
        [first_half * cosine - second * sine_part, second * cosine + first_half * sine_part],
        axis=-1,
    )


def arrival_ranks(sources):
    ordinal = jnp.arange(sources.shape[-1], dtype=jnp.int32)
    earlier = (sources[..., None, :] == sources[..., :, None]) & (
        ordinal[None, :] < ordinal[:, None]
    )
    return jnp.sum(earlier.astype(jnp.int32), axis=-1)


def attend_kernel(parent_ref, length_ref, packed_ref, *refs):
    out_ref = refs[-1]
    group = (len(refs) - 1) // 2
    key_refs = refs[:group]
    value_refs = refs[group : 2 * group]
    step = pl.program_id(0)
    head_width = packed_ref.shape[-1]
    head_total = packed_ref.shape[1] - 2
    @pl.when(length_ref[step * group] == 0)
    def _():
        out_ref[...] = jnp.zeros(out_ref.shape, out_ref.dtype)

    @pl.when(length_ref[step * group] > 0)
    def _():
        for g in range(group):
            length = length_ref[step * group + g]
            attend_one(packed_ref, key_refs[g], value_refs[g], out_ref, g, length, head_total, head_width)


def attend_one(packed_ref, key_ref, value_ref, out_ref, g, length, head_total, head_width):
    score_scale = 1.0 / math.sqrt(head_width)
    if True:
        row = packed_ref[g].astype(jnp.float32)
        queries = row[:head_total].astype(jnp.bfloat16)
        key_new = row[head_total : head_total + 1]
        value_new = row[head_total + 1 : head_total + 2]
        keys_t = key_ref[0]
        values = value_ref[0]
        cached = jnp.dot(queries, keys_t, preferred_element_type=jnp.float32) * score_scale
        latest = (
            jnp.sum(row[:head_total] * key_new, axis=-1, keepdims=True) * score_scale
        )
        slot = lax.broadcasted_iota(jnp.int32, cached.shape, 1)
        cached = jnp.where(slot < length, cached, -jnp.inf)
        highest = jnp.maximum(jnp.max(cached, axis=-1, keepdims=True), latest)
        cached_exp = jnp.exp(cached - highest)
        latest_exp = jnp.exp(latest - highest)
        denominator = jnp.sum(cached_exp, axis=-1, keepdims=True) + latest_exp
        cached_weight = (cached_exp / denominator).astype(jnp.bfloat16)
        latest_weight = (latest_exp / denominator).astype(jnp.bfloat16)
        mixture = jnp.dot(cached_weight, values, preferred_element_type=jnp.float32)
        mixture = mixture + latest_weight.astype(jnp.float32) * value_new
        out_ref[g] = mixture.astype(out_ref.dtype)


def attend_slots(packed, keys_t, values, parents, lengths):
    slot_total, rows, head_width = packed.shape
    head_total = rows - 2
    group = SLOTS_PER_STEP
    cache_len = values.shape[1]

    def cache_map(g):
        return lambda i, parent_ref, length_ref: (parent_ref[i * group + g], 0, 0)

    grid_spec = pltpu.PrefetchScalarGridSpec(
        num_scalar_prefetch=2,
        grid=(slot_total // group,),
        in_specs=[pl.BlockSpec((group, rows, head_width), lambda i, p, l: (i, 0, 0))]
        + [pl.BlockSpec((1, head_width, cache_len), cache_map(g)) for g in range(group)]
        + [pl.BlockSpec((1, cache_len, head_width), cache_map(g)) for g in range(group)],
        out_specs=pl.BlockSpec((group, head_total, head_width), lambda i, p, l: (i, 0, 0)),
    )
    return pl.pallas_call(
        attend_kernel,
        grid_spec=grid_spec,
        out_shape=jax.ShapeDtypeStruct((slot_total, head_total, head_width), jnp.bfloat16),
    )(parents, lengths, packed, *([keys_t] * group), *([values] * group))

def body(
    hidden_in,
    norm_gain,
    query_weight,
    key_weight,
    value_weight,
    output_weight,
    key_value_cache,
    cache_lengths,
    parent_beam,
    beam_alive,
):
    device_count = lax.axis_size(DP)
    device_rank = lax.axis_index(DP)
    local_beams = hidden_in.shape[0]
    capacity = max(2, (2 * local_beams + device_count - 1) // device_count)
    slot_total = device_count * capacity

    hidden_float = hidden_in.astype(jnp.float32)
    inverse = lax.rsqrt(jnp.mean(hidden_float * hidden_float, axis=1) + 1e-06)

    features = query_weight.shape[0]
    pair_count = device_count // 2
    is_low = device_rank % 2 == 0
    partner = [(i, i ^ 1) for i in range(device_count)]
    query_width = query_weight.shape[1]
    key_width = key_weight.shape[1]
    query_half = query_width // 2
    key_half = key_width // 2
    low_cols = jnp.concatenate(
        [query_weight[:, :query_half], key_weight[:, :key_half], value_weight[:, :key_half]],
        axis=1,
    )
    high_cols = jnp.concatenate(
        [query_weight[:, query_half:], key_weight[:, key_half:], value_weight[:, key_half:]],
        axis=1,
    )
    mine = jnp.where(is_low, low_cols, high_cols)
    received = lax.ppermute(jnp.where(is_low, high_cols, low_cols), DP, partner)
    partner_gain = lax.ppermute(norm_gain, DP, partner)
    pair_weight = jnp.where(
        is_low, jnp.concatenate([mine, received], 0), jnp.concatenate([received, mine], 0)
    )
    pair_gain = jnp.where(
        is_low,
        jnp.concatenate([norm_gain, partner_gain]),
        jnp.concatenate([partner_gain, norm_gain]),
    )
    spread = jnp.swapaxes(
        jnp.repeat(hidden_in.reshape(local_beams, pair_count, 2 * features), 2, axis=1), 0, 1
    )
    blocked = lax.all_to_all(spread, DP, 0, 0, tiled=True).reshape(
        device_count * local_beams, 2 * features
    )
    scaled = (blocked.astype(jnp.float32) * pair_gain.astype(jnp.float32)[None, :]).astype(
        jnp.bfloat16
    )
    partial = jnp.dot(scaled, pair_weight, preferred_element_type=jnp.float32)
    half_width = partial.shape[1]
    arrived = lax.all_to_all(
        partial.astype(jnp.bfloat16).reshape(device_count, local_beams, half_width),
        DP,
        0,
        0,
        tiled=True,
    )
    sums = jnp.sum(
        arrived.astype(jnp.float32).reshape(pair_count, 2, local_beams, half_width), axis=0
    )
    key_end = query_half + key_half
    summed = jnp.concatenate(
        [
            sums[0, :, :query_half],
            sums[1, :, :query_half],
            sums[0, :, query_half:key_end],
            sums[1, :, query_half:key_end],
            sums[0, :, key_end:],
            sums[1, :, key_end:],
        ],
        axis=1,
    ) * inverse[:, None]
    keys_t = jnp.swapaxes(key_value_cache[:, :, 0, 0, :], 1, 2)
    values = key_value_cache[:, :, 1, 0, :]
    summed, keys_t, values = lax.optimization_barrier((summed, keys_t, values))

    first_beam = device_rank * local_beams
    my_parent = lax.dynamic_slice_in_dim(parent_beam, first_beam, local_beams)
    my_alive = lax.dynamic_slice_in_dim(beam_alive, first_beam, local_beams)
    position = jnp.take(cache_lengths, my_parent)
    head_count = query_width // HEAD_DIM
    group_count = key_width // HEAD_DIM
    queries = rotate(
        summed[:, :query_width].reshape(local_beams, head_count, HEAD_DIM), position
    ).astype(jnp.bfloat16)
    key_new = rotate(
        summed[:, query_width : query_width + key_width].reshape(
            local_beams, group_count, HEAD_DIM
        ),
        position,
    ).astype(jnp.bfloat16)
    value_new = (
        summed[:, query_width + key_width :]
        .reshape(local_beams, group_count, HEAD_DIM)
        .astype(jnp.bfloat16)
    )
    packed = jnp.concatenate([queries, key_new, value_new], axis=1)
    rows = packed.shape[1]

    source = my_parent // local_beams
    target = source * capacity + arrival_ranks(source)
    slot_of = jnp.arange(slot_total, dtype=jnp.int32)
    match = target[None, :] == slot_of[:, None]
    filled = jnp.any(match, axis=1)
    sender = jnp.argmax(match, axis=1)
    outgoing = jnp.where(
        filled[:, None, None], jnp.take(packed, sender, axis=0), jnp.zeros_like(packed[:1])
    )
    incoming = lax.all_to_all(
        outgoing.reshape(device_count, capacity, rows, HEAD_DIM), DP, 0, 0, tiled=True
    ).reshape(slot_total, rows, HEAD_DIM)

    all_parents = parent_beam.reshape(device_count, local_beams)
    all_sources = all_parents // local_beams
    destination = jnp.broadcast_to(
        jnp.arange(device_count, dtype=jnp.int32)[:, None], (device_count, local_beams)
    )
    placed = jnp.where(
        all_sources == device_rank, destination * capacity + arrival_ranks(all_sources), slot_total
    )
    chosen = placed.reshape(-1)[None, :] == slot_of[:, None]
    local_parent = jnp.sum(
        jnp.where(chosen, (all_parents % local_beams).reshape(-1)[None, :], 0), axis=1
    )
    used = jnp.any(chosen, axis=1).astype(jnp.int32)
    slot_length = jnp.take(cache_lengths, first_beam + local_parent) * used

    real_rank = jnp.cumsum(used) - 1
    pad_rank = jnp.sum(used) + jnp.cumsum(1 - used) - 1
    order = jnp.where(used > 0, real_rank, pad_rank)
    moved = order[None, :] == slot_of[:, None]
    sorted_from = jnp.sum(jnp.where(moved, slot_of[None, :], 0), axis=1)
    mixed_sorted = attend_slots(
        jnp.take(incoming, sorted_from, axis=0),
        keys_t,
        values,
        jnp.take(local_parent, sorted_from),
        jnp.take(slot_length, sorted_from),
    )
    mixed = jnp.take(mixed_sorted, order, axis=0)
    returned = lax.all_to_all(
        mixed.reshape(device_count, capacity, head_count * HEAD_DIM), DP, 0, 0, tiled=True
    ).reshape(slot_total, head_count * HEAD_DIM)
    attention = jnp.take(returned, target, axis=0)
    attention = jnp.where(my_alive[:, None] > 0, attention, jnp.zeros_like(attention))

    z_count = lax.axis_size("dz")
    y_count = lax.axis_size("dy")
    along_z = lax.all_to_all(
        jnp.broadcast_to(attention[None], (z_count,) + attention.shape), "dz", 0, 0, tiled=True
    ).reshape(z_count * local_beams, head_count * HEAD_DIM)
    gathered = lax.all_to_all(
        jnp.broadcast_to(along_z[None], (y_count,) + along_z.shape), "dy", 0, 0, tiled=True
    ).reshape(device_count * local_beams, head_count * HEAD_DIM)
    partial_sum = jnp.dot(gathered, output_weight, preferred_element_type=jnp.float32)
    total_rows, out_width = partial_sum.shape
    core_count = lax.axis_size("tc")
    ring_count = lax.axis_size("tx")
    on_chip = jnp.sum(
        lax.all_to_all(
            partial_sum.reshape(core_count, total_rows // core_count, out_width), "tc", 0, 0, tiled=True
        ),
        axis=0,
    )
    chunk_rows = total_rows // (core_count * ring_count)
    reduced = jnp.sum(
        lax.all_to_all(on_chip.reshape(ring_count, chunk_rows, out_width), "tx", 0, 0, tiled=True),
        axis=0,
    ).astype(jnp.bfloat16)
    ring_copies = lax.all_to_all(
        jnp.broadcast_to(reduced[None], (ring_count,) + reduced.shape), "tx", 0, 0, tiled=True
    ).reshape(ring_count * chunk_rows, out_width)
    return lax.all_to_all(
        jnp.broadcast_to(ring_copies[None], (core_count,) + ring_copies.shape), "tc", 0, 0, tiled=True
    ).reshape(total_rows, out_width)

def solution(mesh):
    y_count = PLANE_Y
    devices = mesh.devices.reshape(y_count, mesh.devices.shape[0] // y_count, -1, 2)
    mesh = jax.sharding.Mesh(devices, ("dy", "dz", "tx", "tc"))
    placed = (
        P(DP, None),
        P(DP),
        P(DP, TP),
        P(DP, TP),
        P(DP, TP),
        P(TP, DP),
        P(DP, None, None, TP, None),
        P(),
        P(),
        P(),
    )
    return jax.shard_map(body, mesh=mesh, in_specs=placed, out_specs=P(None, DP), check_vma=False)
```

```python
import functools
import math

import jax
import jax.numpy as jnp
from jax import lax
from jax.experimental import pallas as pl
from jax.experimental.pallas import tpu as pltpu
from jax.sharding import PartitionSpec as P

HEAD_DIM = 128
SLOTS_PER_STEP = 16
PLANE_Y = 4
DP = ("dy", "dz")
TP = ("tx", "tc")


def rotate(vectors, position):
    half_width = vectors.shape[-1] // 2
    pair_index = jnp.arange(half_width).astype(jnp.float32)
    frequency = jnp.exp(pair_index * (-2.0 * math.log(1000000.0) / vectors.shape[-1]))
    angles = position.astype(jnp.float32)[:, None] * frequency[None, :]
    cosine = jnp.cos(angles)[:, None, :]
    sine_part = jnp.sin(angles)[:, None, :]
    first_half = vectors[..., :half_width]
    second = vectors[..., half_width:]
    return jnp.concatenate(
        [first_half * cosine - second * sine_part, second * cosine + first_half * sine_part],
        axis=-1,
    )


def arrival_ranks(sources):
    ordinal = jnp.arange(sources.shape[-1], dtype=jnp.int32)
    earlier = (sources[..., None, :] == sources[..., :, None]) & (
        ordinal[None, :] < ordinal[:, None]
    )
    return jnp.sum(earlier.astype(jnp.int32), axis=-1)


def attend_kernel(parent_ref, length_ref, packed_ref, *refs):
    out_ref = refs[-1]
    group = (len(refs) - 1) // 2
    key_refs = refs[:group]
    value_refs = refs[group : 2 * group]
    step = pl.program_id(0)
    head_width = packed_ref.shape[-1]
    head_total = packed_ref.shape[1] - 2
    @pl.when(length_ref[step * group] == 0)
    def _():
        out_ref[...] = jnp.zeros(out_ref.shape, out_ref.dtype)

    @pl.when(length_ref[step * group] > 0)
    def _():
        for g in range(group):
            length = length_ref[step * group + g]
            attend_one(packed_ref, key_refs[g], value_refs[g], out_ref, g, length, head_total, head_width)


def attend_one(packed_ref, key_ref, value_ref, out_ref, g, length, head_total, head_width):
    score_scale = 1.0 / math.sqrt(head_width)
    if True:
        row = packed_ref[g].astype(jnp.float32)
        queries = row[:head_total].astype(jnp.bfloat16)
        key_new = row[head_total : head_total + 1]
        value_new = row[head_total + 1 : head_total + 2]
        keys_t = key_ref[0]
        values = value_ref[0]
        cached = jnp.dot(queries, keys_t, preferred_element_type=jnp.float32) * score_scale
        latest = (
            jnp.sum(row[:head_total] * key_new, axis=-1, keepdims=True) * score_scale
        )
        slot = lax.broadcasted_iota(jnp.int32, cached.shape, 1)
        cached = jnp.where(slot < length, cached, -jnp.inf)
        highest = jnp.maximum(jnp.max(cached, axis=-1, keepdims=True), latest)
        cached_exp = jnp.exp(cached - highest)
        latest_exp = jnp.exp(latest - highest)
        denominator = jnp.sum(cached_exp, axis=-1, keepdims=True) + latest_exp
        cached_weight = (cached_exp / denominator).astype(jnp.bfloat16)
        latest_weight = (latest_exp / denominator).astype(jnp.bfloat16)
        mixture = jnp.dot(cached_weight, values, preferred_element_type=jnp.float32)
        mixture = mixture + latest_weight.astype(jnp.float32) * value_new
        out_ref[g] = mixture.astype(out_ref.dtype)


def attend_slots(packed, keys_t, values, parents, lengths):
    slot_total, rows, head_width = packed.shape
    head_total = rows - 2
    group = SLOTS_PER_STEP
    cache_len = values.shape[1]

    def cache_map(g):
        return lambda i, parent_ref, length_ref: (parent_ref[i * group + g], 0, 0)

    grid_spec = pltpu.PrefetchScalarGridSpec(
        num_scalar_prefetch=2,
        grid=(slot_total // group,),
        in_specs=[pl.BlockSpec((group, rows, head_width), lambda i, p, l: (i, 0, 0))]
        + [pl.BlockSpec((1, head_width, cache_len), cache_map(g)) for g in range(group)]
        + [pl.BlockSpec((1, cache_len, head_width), cache_map(g)) for g in range(group)],
        out_specs=pl.BlockSpec((group, head_total, head_width), lambda i, p, l: (i, 0, 0)),
    )
    return pl.pallas_call(
        attend_kernel,
        grid_spec=grid_spec,
        out_shape=jax.ShapeDtypeStruct((slot_total, head_total, head_width), jnp.bfloat16),
    )(parents, lengths, packed, *([keys_t] * group), *([values] * group))

def body(
    hidden_in,
    norm_gain,
    query_weight,
    key_weight,
    value_weight,
    output_weight,
    key_value_cache,
    cache_lengths,
    parent_beam,
    beam_alive,
):
    device_count = lax.axis_size(DP)
    device_rank = lax.axis_index(DP)
    local_beams = hidden_in.shape[0]
    capacity = max(2, (2 * local_beams + device_count - 1) // device_count)
    slot_total = device_count * capacity

    hidden_float = hidden_in.astype(jnp.float32)
    inverse = lax.rsqrt(jnp.mean(hidden_float * hidden_float, axis=1) + 1e-06)

    features = query_weight.shape[0]
    pair_count = device_count // 2
    is_low = device_rank % 2 == 0
    partner = [(i, i ^ 1) for i in range(device_count)]
    query_width = query_weight.shape[1]
    key_width = key_weight.shape[1]
    query_half = query_width // 2
    key_half = key_width // 2
    low_cols = jnp.concatenate(
        [query_weight[:, :query_half], key_weight[:, :key_half], value_weight[:, :key_half]],
        axis=1,
    )
    high_cols = jnp.concatenate(
        [query_weight[:, query_half:], key_weight[:, key_half:], value_weight[:, key_half:]],
        axis=1,
    )
    mine = jnp.where(is_low, low_cols, high_cols)
    received = lax.ppermute(jnp.where(is_low, high_cols, low_cols), DP, partner)
    partner_gain = lax.ppermute(norm_gain, DP, partner)
    pair_weight = jnp.where(
        is_low, jnp.concatenate([mine, received], 0), jnp.concatenate([received, mine], 0)
    )
    pair_gain = jnp.where(
        is_low,
        jnp.concatenate([norm_gain, partner_gain]),
        jnp.concatenate([partner_gain, norm_gain]),
    )
    spread = jnp.swapaxes(
        jnp.repeat(hidden_in.reshape(local_beams, pair_count, 2 * features), 2, axis=1), 0, 1
    )
    blocked = lax.all_to_all(spread, DP, 0, 0, tiled=True).reshape(
        device_count * local_beams, 2 * features
    )
    scaled = (blocked.astype(jnp.float32) * pair_gain.astype(jnp.float32)[None, :]).astype(
        jnp.bfloat16
    )
    partial = jnp.dot(scaled, pair_weight, preferred_element_type=jnp.float32)
    half_width = partial.shape[1]
    arrived = lax.all_to_all(
        partial.astype(jnp.bfloat16).reshape(device_count, local_beams, half_width),
        DP,
        0,
        0,
        tiled=True,
    )
    sums = jnp.sum(
        arrived.astype(jnp.float32).reshape(pair_count, 2, local_beams, half_width), axis=0
    )
    key_end = query_half + key_half
    summed = jnp.concatenate(
        [
            sums[0, :, :query_half],
            sums[1, :, :query_half],
            sums[0, :, query_half:key_end],
            sums[1, :, query_half:key_end],
            sums[0, :, key_end:],
            sums[1, :, key_end:],
        ],
        axis=1,
    ) * inverse[:, None]
    keys_t = jnp.swapaxes(key_value_cache[:, :, 0, 0, :], 1, 2)
    values = key_value_cache[:, :, 1, 0, :]
    summed, keys_t, values = lax.optimization_barrier((summed, keys_t, values))

    first_beam = device_rank * local_beams
    my_parent = lax.dynamic_slice_in_dim(parent_beam, first_beam, local_beams)
    my_alive = lax.dynamic_slice_in_dim(beam_alive, first_beam, local_beams)
    position = jnp.take(cache_lengths, my_parent)
    head_count = query_width // HEAD_DIM
    group_count = key_width // HEAD_DIM
    queries = rotate(
        summed[:, :query_width].reshape(local_beams, head_count, HEAD_DIM), position
    ).astype(jnp.bfloat16)
    key_new = rotate(
        summed[:, query_width : query_width + key_width].reshape(
            local_beams, group_count, HEAD_DIM
        ),
        position,
    ).astype(jnp.bfloat16)
    value_new = (
        summed[:, query_width + key_width :]
        .reshape(local_beams, group_count, HEAD_DIM)
        .astype(jnp.bfloat16)
    )
    packed = jnp.concatenate([queries, key_new, value_new], axis=1)
    rows = packed.shape[1]

    source = my_parent // local_beams
    target = source * capacity + arrival_ranks(source)
    slot_of = jnp.arange(slot_total, dtype=jnp.int32)
    match = target[None, :] == slot_of[:, None]
    filled = jnp.any(match, axis=1)
    sender = jnp.argmax(match, axis=1)
    outgoing = jnp.where(
        filled[:, None, None], jnp.take(packed, sender, axis=0), jnp.zeros_like(packed[:1])
    )
    incoming = lax.all_to_all(
        outgoing.reshape(device_count, capacity, rows, HEAD_DIM), DP, 0, 0, tiled=True
    ).reshape(slot_total, rows, HEAD_DIM)

    all_parents = parent_beam.reshape(device_count, local_beams)
    all_sources = all_parents // local_beams
    destination = jnp.broadcast_to(
        jnp.arange(device_count, dtype=jnp.int32)[:, None], (device_count, local_beams)
    )
    placed = jnp.where(
        all_sources == device_rank, destination * capacity + arrival_ranks(all_sources), slot_total
    )
    chosen = placed.reshape(-1)[None, :] == slot_of[:, None]
    local_parent = jnp.sum(
        jnp.where(chosen, (all_parents % local_beams).reshape(-1)[None, :], 0), axis=1
    )
    used = jnp.any(chosen, axis=1).astype(jnp.int32)
    slot_length = jnp.take(cache_lengths, first_beam + local_parent) * used

    real_rank = jnp.cumsum(used) - 1
    pad_rank = jnp.sum(used) + jnp.cumsum(1 - used) - 1
    order = jnp.where(used > 0, real_rank, pad_rank)
    moved = order[None, :] == slot_of[:, None]
    sorted_from = jnp.sum(jnp.where(moved, slot_of[None, :], 0), axis=1)
    mixed_sorted = attend_slots(
        jnp.take(incoming, sorted_from, axis=0),
        keys_t,
        values,
        jnp.take(local_parent, sorted_from),
        jnp.take(slot_length, sorted_from),
    )
    mixed = jnp.take(mixed_sorted, order, axis=0)
    returned = lax.all_to_all(
        mixed.reshape(device_count, capacity, head_count * HEAD_DIM), DP, 0, 0, tiled=True
    ).reshape(slot_total, head_count * HEAD_DIM)
    attention = jnp.take(returned, target, axis=0)
    attention = jnp.where(my_alive[:, None] > 0, attention, jnp.zeros_like(attention))

    z_count = lax.axis_size("dz")
    y_count = lax.axis_size("dy")
    along_z = lax.all_to_all(
        jnp.broadcast_to(attention[None], (z_count,) + attention.shape), "dz", 0, 0, tiled=True
    ).reshape(z_count * local_beams, head_count * HEAD_DIM)
    gathered = lax.all_to_all(
        jnp.broadcast_to(along_z[None], (y_count,) + along_z.shape), "dy", 0, 0, tiled=True
    ).reshape(device_count * local_beams, head_count * HEAD_DIM)
    partial_sum = jnp.dot(gathered, output_weight, preferred_element_type=jnp.float32)
    total_rows, out_width = partial_sum.shape
    core_count = lax.axis_size("tc")
    ring_count = lax.axis_size("tx")
    on_chip = jnp.sum(
        lax.all_to_all(
            partial_sum.reshape(core_count, total_rows // core_count, out_width), "tc", 0, 0, tiled=True
        ),
        axis=0,
    )
    chunk_rows = total_rows // (core_count * ring_count)
    reduced = jnp.sum(
        lax.all_to_all(on_chip.reshape(ring_count, chunk_rows, out_width), "tx", 0, 0, tiled=True),
        axis=0,
    ).astype(jnp.bfloat16)
    copies = lax.all_to_all(
        jnp.broadcast_to(reduced[None], (ring_count * core_count,) + reduced.shape), TP, 0, 0, tiled=True
    )
    return jnp.swapaxes(
        copies.reshape(ring_count, core_count, chunk_rows, out_width), 0, 1
    ).reshape(total_rows, out_width)

def solution(mesh):
    y_count = PLANE_Y
    devices = mesh.devices.reshape(y_count, mesh.devices.shape[0] // y_count, -1, 2)
    mesh = jax.sharding.Mesh(devices, ("dy", "dz", "tx", "tc"))
    placed = (
        P(DP, None),
        P(DP),
        P(DP, TP),
        P(DP, TP),
        P(DP, TP),
        P(TP, DP),
        P(DP, None, None, TP, None),
        P(),
        P(),
        P(),
    )
    return jax.shard_map(body, mesh=mesh, in_specs=placed, out_specs=P(None, DP), check_vma=False)
```

```python
import functools
import math

import jax
import jax.numpy as jnp
from jax import lax
from jax.experimental import pallas as pl
from jax.experimental.pallas import tpu as pltpu
from jax.sharding import PartitionSpec as P

HEAD_DIM = 128
SLOTS_PER_STEP = 16
PLANE_Y = 4
DP = ("dy", "dz")
TP = ("tx", "tc")


def rotate(vectors, position):
    half_width = vectors.shape[-1] // 2
    pair_index = jnp.arange(half_width).astype(jnp.float32)
    frequency = jnp.exp(pair_index * (-2.0 * math.log(1000000.0) / vectors.shape[-1]))
    angles = position.astype(jnp.float32)[:, None] * frequency[None, :]
    cosine = jnp.cos(angles)[:, None, :]
    sine_part = jnp.sin(angles)[:, None, :]
    first_half = vectors[..., :half_width]
    second = vectors[..., half_width:]
    return jnp.concatenate(
        [first_half * cosine - second * sine_part, second * cosine + first_half * sine_part],
        axis=-1,
    )


def arrival_ranks(sources):
    ordinal = jnp.arange(sources.shape[-1], dtype=jnp.int32)
    earlier = (sources[..., None, :] == sources[..., :, None]) & (
        ordinal[None, :] < ordinal[:, None]
    )
    return jnp.sum(earlier.astype(jnp.int32), axis=-1)


def attend_kernel(parent_ref, length_ref, packed_ref, *refs):
    out_ref = refs[-1]
    group = (len(refs) - 1) // 2
    key_refs = refs[:group]
    value_refs = refs[group : 2 * group]
    step = pl.program_id(0)
    head_width = packed_ref.shape[-1]
    head_total = packed_ref.shape[1] - 2
    @pl.when(length_ref[step * group] == 0)
    def _():
        out_ref[...] = jnp.zeros(out_ref.shape, out_ref.dtype)

    @pl.when(length_ref[step * group] > 0)
    def _():
        for g in range(group):
            length = length_ref[step * group + g]
            attend_one(packed_ref, key_refs[g], value_refs[g], out_ref, g, length, head_total, head_width)


def attend_one(packed_ref, key_ref, value_ref, out_ref, g, length, head_total, head_width):
    score_scale = 1.0 / math.sqrt(head_width)
    if True:
        row = packed_ref[g].astype(jnp.float32)
        queries = row[:head_total].astype(jnp.bfloat16)
        key_new = row[head_total : head_total + 1]
        value_new = row[head_total + 1 : head_total + 2]
        keys_t = key_ref[0]
        values = value_ref[0]
        cached = jnp.dot(queries, keys_t, preferred_element_type=jnp.float32) * score_scale
        latest = (
            jnp.sum(row[:head_total] * key_new, axis=-1, keepdims=True) * score_scale
        )
        slot = lax.broadcasted_iota(jnp.int32, cached.shape, 1)
        cached = jnp.where(slot < length, cached, -jnp.inf)
        highest = jnp.maximum(jnp.max(cached, axis=-1, keepdims=True), latest)
        cached_exp = jnp.exp(cached - highest)
        latest_exp = jnp.exp(latest - highest)
        denominator = jnp.sum(cached_exp, axis=-1, keepdims=True) + latest_exp
        cached_weight = (cached_exp / denominator).astype(jnp.bfloat16)
        latest_weight = (latest_exp / denominator).astype(jnp.bfloat16)
        mixture = jnp.dot(cached_weight, values, preferred_element_type=jnp.float32)
        mixture = mixture + latest_weight.astype(jnp.float32) * value_new
        out_ref[g] = mixture.astype(out_ref.dtype)


def attend_slots(packed, keys_t, values, parents, lengths):
    slot_total, rows, head_width = packed.shape
    head_total = rows - 2
    group = SLOTS_PER_STEP
    cache_len = values.shape[1]

    def cache_map(g):
        return lambda i, parent_ref, length_ref: (parent_ref[i * group + g], 0, 0)

    grid_spec = pltpu.PrefetchScalarGridSpec(
        num_scalar_prefetch=2,
        grid=(slot_total // group,),
        in_specs=[pl.BlockSpec((group, rows, head_width), lambda i, p, l: (i, 0, 0))]
        + [pl.BlockSpec((1, head_width, cache_len), cache_map(g)) for g in range(group)]
        + [pl.BlockSpec((1, cache_len, head_width), cache_map(g)) for g in range(group)],
        out_specs=pl.BlockSpec((group, head_total, head_width), lambda i, p, l: (i, 0, 0)),
    )
    return pl.pallas_call(
        attend_kernel,
        grid_spec=grid_spec,
        out_shape=jax.ShapeDtypeStruct((slot_total, head_total, head_width), jnp.bfloat16),
    )(parents, lengths, packed, *([keys_t] * group), *([values] * group))

def body(
    hidden_in,
    norm_gain,
    query_weight,
    key_weight,
    value_weight,
    output_weight,
    key_value_cache,
    cache_lengths,
    parent_beam,
    beam_alive,
):
    device_count = lax.axis_size(DP)
    device_rank = lax.axis_index(DP)
    local_beams = hidden_in.shape[0]
    capacity = max(2, (2 * local_beams + device_count - 1) // device_count)
    slot_total = device_count * capacity

    hidden_float = hidden_in.astype(jnp.float32)
    inverse = lax.rsqrt(jnp.mean(hidden_float * hidden_float, axis=1) + 1e-06)

    features = query_weight.shape[0]
    pair_count = device_count // 2
    is_low = device_rank % 2 == 0
    partner = [(i, i ^ 1) for i in range(device_count)]
    query_width = query_weight.shape[1]
    key_width = key_weight.shape[1]
    query_half = query_width // 2
    key_half = key_width // 2
    low_cols = jnp.concatenate(
        [query_weight[:, :query_half], key_weight[:, :key_half], value_weight[:, :key_half]],
        axis=1,
    )
    high_cols = jnp.concatenate(
        [query_weight[:, query_half:], key_weight[:, key_half:], value_weight[:, key_half:]],
        axis=1,
    )
    mine = jnp.where(is_low, low_cols, high_cols)
    received = lax.ppermute(jnp.where(is_low, high_cols, low_cols), DP, partner)
    partner_gain = lax.ppermute(norm_gain, DP, partner)
    pair_weight = jnp.where(
        is_low, jnp.concatenate([mine, received], 0), jnp.concatenate([received, mine], 0)
    )
    pair_gain = jnp.where(
        is_low,
        jnp.concatenate([norm_gain, partner_gain]),
        jnp.concatenate([partner_gain, norm_gain]),
    )
    spread = jnp.swapaxes(
        jnp.repeat(hidden_in.reshape(local_beams, pair_count, 2 * features), 2, axis=1), 0, 1
    )
    blocked = lax.all_to_all(spread, DP, 0, 0, tiled=True).reshape(
        device_count * local_beams, 2 * features
    )
    scaled = (blocked.astype(jnp.float32) * pair_gain.astype(jnp.float32)[None, :]).astype(
        jnp.bfloat16
    )
    partial = jnp.dot(scaled, pair_weight, preferred_element_type=jnp.float32)
    half_width = partial.shape[1]
    arrived = lax.all_to_all(
        partial.astype(jnp.bfloat16).reshape(device_count, local_beams, half_width),
        DP,
        0,
        0,
        tiled=True,
    )
    sums = jnp.sum(
        arrived.astype(jnp.float32).reshape(pair_count, 2, local_beams, half_width), axis=0
    )
    key_end = query_half + key_half
    summed = jnp.concatenate(
        [
            sums[0, :, :query_half],
            sums[1, :, :query_half],
            sums[0, :, query_half:key_end],
            sums[1, :, query_half:key_end],
            sums[0, :, key_end:],
            sums[1, :, key_end:],
        ],
        axis=1,
    ) * inverse[:, None]
    keys_t = jnp.swapaxes(key_value_cache[:, :, 0, 0, :], 1, 2)
    values = key_value_cache[:, :, 1, 0, :]
    summed, keys_t, values = lax.optimization_barrier((summed, keys_t, values))

    first_beam = device_rank * local_beams
    my_parent = lax.dynamic_slice_in_dim(parent_beam, first_beam, local_beams)
    my_alive = lax.dynamic_slice_in_dim(beam_alive, first_beam, local_beams)
    position = jnp.take(cache_lengths, my_parent)
    head_count = query_width // HEAD_DIM
    group_count = key_width // HEAD_DIM
    queries = rotate(
        summed[:, :query_width].reshape(local_beams, head_count, HEAD_DIM), position
    ).astype(jnp.bfloat16)
    key_new = rotate(
        summed[:, query_width : query_width + key_width].reshape(
            local_beams, group_count, HEAD_DIM
        ),
        position,
    ).astype(jnp.bfloat16)
    value_new = (
        summed[:, query_width + key_width :]
        .reshape(local_beams, group_count, HEAD_DIM)
        .astype(jnp.bfloat16)
    )
    packed = jnp.concatenate([queries, key_new, value_new], axis=1)
    rows = packed.shape[1]

    source = my_parent // local_beams
    target = source * capacity + arrival_ranks(source)
    slot_of = jnp.arange(slot_total, dtype=jnp.int32)
    match = target[None, :] == slot_of[:, None]
    filled = jnp.any(match, axis=1)
    sender = jnp.argmax(match, axis=1)
    outgoing = jnp.where(
        filled[:, None, None], jnp.take(packed, sender, axis=0), jnp.zeros_like(packed[:1])
    )
    incoming = lax.all_to_all(
        outgoing.reshape(device_count, capacity, rows, HEAD_DIM), DP, 0, 0, tiled=True
    ).reshape(slot_total, rows, HEAD_DIM)

    all_parents = parent_beam.reshape(device_count, local_beams)
    all_sources = all_parents // local_beams
    destination = jnp.broadcast_to(
        jnp.arange(device_count, dtype=jnp.int32)[:, None], (device_count, local_beams)
    )
    placed = jnp.where(
        all_sources == device_rank, destination * capacity + arrival_ranks(all_sources), slot_total
    )
    chosen = placed.reshape(-1)[None, :] == slot_of[:, None]
    local_parent = jnp.sum(
        jnp.where(chosen, (all_parents % local_beams).reshape(-1)[None, :], 0), axis=1
    )
    used = jnp.any(chosen, axis=1).astype(jnp.int32)
    slot_length = jnp.take(cache_lengths, first_beam + local_parent) * used

    real_rank = jnp.cumsum(used) - 1
    pad_rank = jnp.sum(used) + jnp.cumsum(1 - used) - 1
    order = jnp.where(used > 0, real_rank, pad_rank)
    moved = order[None, :] == slot_of[:, None]
    sorted_from = jnp.sum(jnp.where(moved, slot_of[None, :], 0), axis=1)
    mixed_sorted = attend_slots(
        jnp.take(incoming, sorted_from, axis=0),
        keys_t,
        values,
        jnp.take(local_parent, sorted_from),
        jnp.take(slot_length, sorted_from),
    )
    mixed = jnp.take(mixed_sorted, order, axis=0)
    returned = lax.all_to_all(
        mixed.reshape(device_count, capacity, head_count * HEAD_DIM), DP, 0, 0, tiled=True
    ).reshape(slot_total, head_count * HEAD_DIM)
    attention = jnp.take(returned, target, axis=0)
    attention = jnp.where(my_alive[:, None] > 0, attention, jnp.zeros_like(attention))

    z_count = lax.axis_size("dz")
    y_count = lax.axis_size("dy")
    along_z = lax.all_to_all(
        jnp.broadcast_to(attention[None], (z_count,) + attention.shape), "dz", 0, 0, tiled=True
    ).reshape(z_count * local_beams, head_count * HEAD_DIM)
    gathered = lax.all_to_all(
        jnp.broadcast_to(along_z[None], (y_count,) + along_z.shape), "dy", 0, 0, tiled=True
    ).reshape(device_count * local_beams, head_count * HEAD_DIM)
    partial_sum = jnp.dot(gathered, output_weight, preferred_element_type=jnp.float32)
    total_rows, out_width = partial_sum.shape
    core_count = lax.axis_size("tc")
    ring_count = lax.axis_size("tx")
    group_size = core_count * ring_count
    chunk_rows = total_rows // group_size
    reduced = jnp.sum(
        lax.all_to_all(partial_sum.reshape(group_size, chunk_rows, out_width), TP, 0, 0, tiled=True),
        axis=0,
    ).astype(jnp.bfloat16)
    return lax.all_to_all(
        jnp.broadcast_to(reduced[None], (group_size,) + reduced.shape), TP, 0, 0, tiled=True
    ).reshape(total_rows, out_width)

def solution(mesh):
    y_count = PLANE_Y
    devices = mesh.devices.reshape(y_count, mesh.devices.shape[0] // y_count, -1, 2)
    mesh = jax.sharding.Mesh(devices, ("dy", "dz", "tx", "tc"))
    placed = (
        P(DP, None),
        P(DP),
        P(DP, TP),
        P(DP, TP),
        P(DP, TP),
        P(TP, DP),
        P(DP, None, None, TP, None),
        P(),
        P(),
        P(),
    )
    return jax.shard_map(body, mesh=mesh, in_specs=placed, out_specs=P(None, DP), check_vma=False)
```
